32 devices in a mesh: groups: 2 (over y), fsdp: 4 (over z), segment: 4 (over x, core).
Axes of the slice: x: 2, y: 2, z: 4, core: 2. Of those that a mesh axis runs over, the one named last changes fastest.
Arguments:
- layer_inputs: bfloat16 [32, 8192], P(('groups', 'fsdp'), 'segment'), parts along dimension 0, may hold values from -6 to 6
- labels: int32 [32], P('groups'), parts along dimension 0, may hold values from 0 to 1
- head_weight: float32 [4096], replicated, may hold values from -5 to 5
- gate_up_store: bfloat16 [1280, 4, 2, 128, 128], P('fsdp', 'segment'), may hold values from -0.125 to 0.125
- down_store: bfloat16 [1280, 4, 128, 128], P('fsdp', 'segment'), may hold values from -0.0625 to 0.0625
- kept_rows: int32 [2, 128, 16], replicated, may hold values from 0 to 31, as said below
- owners: int32 [2, 128, 16], replicated, may hold values from 0 to 3, as said below
- slots: int32 [2, 128, 16], replicated, may hold values from 0 to 319, as said below
Outputs:
- input_grads: bfloat16 [32, 8192], P(('groups', 'fsdp'), 'segment'), parts along dimension 0
- gate_up_grads: bfloat16 [2560, 4, 2, 128, 128], P(('groups', 'fsdp'), 'segment'), parts along dimension 0
- down_grads: bfloat16 [2560, 4, 128, 128], P(('groups', 'fsdp'), 'segment'), parts along dimension 0
The draws below stay inside these ranges and needn't reach their ends.
There are 2 independent parts, one for each index of `groups`. The reference program is written for one: setup_inputs(seed, part) draws one part's arguments, and reference() takes and returns one part's arrays. A program takes and returns all parts, laid end to end along the dimension named above; an argument that names none is the same for every part. Nothing has to cross between parts.
Inputs may be any that keep to these rules, and one draw needn't show every extreme that they name: kept_rows[p, j] holds 16 distinct block rows. `owners`: call (j // 16) mod 4 the reader of hidden block column j. For each segment p and each value of j // 64, one fsdp index stores at most 320 of those kept blocks, and at most 80 of them with one reader; both bounds are reached. Kept blocks with the same segment, the same j // 64 and the same owner have distinct slots.
All inputs are finite; a program needn't handle non-finite values.
Results may differ from the reference program's by a relative error of at most 0.008.
Values may be sent and summed in bfloat16 or wider, within the bound.
No kernel may reach another device: no remote copies, remote signals or barrier semaphores. Data moves between devices by JAX's collectives and lax.ppermute only.
A program may use at most 256 MiB of HBM per device.

```python
import jax
import jax.numpy as jnp
from jax import lax

D = 4096
FF = 16384
BLK = 128
PIPE = 2
TOKENS = 16
COLS = 16
CAP = 320
N_FSDP = 4
N_SEGMENT = 4


def block_layout(key):
    nrow = D // BLK
    kept = nrow // 2
    ncols = FF // BLK
    sections = N_SEGMENT // PIPE
    cols = ncols // (N_FSDP * sections)
    reach = cols * kept
    quarter = reach // 4
    row_key = jax.random.fold_in(key, 101)
    row_keys = jax.random.split(row_key, PIPE * ncols)
    orders = jax.vmap(lambda item: jax.random.permutation(item, nrow))(row_keys)
    rows = orders[:, :kept].astype(jnp.int32).reshape(PIPE, ncols, kept)
    owner_key = jax.random.fold_in(key, 202)
    group_keys = jax.random.split(owner_key, PIPE * sections)
    positions = jnp.arange(N_FSDP, dtype=jnp.int32)[:, None] + N_FSDP * jnp.arange(reach, dtype=jnp.int32)[None, :]

    def one_group(group_key):
        load_key, label_key = jax.random.split(group_key)
        shifts = jax.random.randint(load_key, (N_FSDP // 2,), 0, quarter + 1).astype(jnp.int32)
        shifts = shifts.at[0].set(quarter)
        loads = jnp.stack([reach + shifts, reach - shifts], axis=1).reshape(N_FSDP)
        ends = jnp.cumsum(loads)
        starts = ends - loads
        owner_id = jnp.sum((ends[None, None, :] <= positions[:, :, None]).astype(jnp.int32), axis=2)
        slot = positions - starts[owner_id]
        labels_map = jax.random.permutation(label_key, N_FSDP).astype(jnp.int32)
        return (labels_map[owner_id], slot)
    owner_all, slot_all = jax.vmap(one_group)(group_keys)
    owner_all = owner_all.reshape(PIPE, ncols, kept).astype(jnp.int32)
    slot_all = slot_all.reshape(PIPE, ncols, kept).astype(jnp.int32)
    return (rows, owner_all, slot_all)


def draw_kept_rows(key, part):
    return block_layout(key)[0]


def draw_owners(key, part):
    return block_layout(key)[1]


def draw_slots(key, part):
    return block_layout(key)[2]


def plant(array, key, least, high):
    longest = array.shape.index(max(array.shape))
    spots = []
    for shift in (0, 1):
        where = [jax.random.randint(jax.random.fold_in(key, axis), (), 0, length) for axis, length in enumerate(array.shape)]
        where[longest] = (where[longest] + shift) % array.shape[longest]
        spots.append(tuple(where))
    return array.at[spots[0]].set(least).at[spots[1]].set(high)


def block_levels(own_key, shape, shards, low, largest):
    def one(axis_at, shards_of):
        steps = jax.random.uniform(jax.random.fold_in(jax.random.fold_in(own_key, 6), axis_at), (shards_of,), jnp.float32, low / len(shards), largest / len(shards))
        return jnp.repeat(jnp.exp(steps), shape[axis_at] // shards_of).reshape((-1,) + (1,) * (len(shape) - axis_at - 1))

    factor_of = one(*shards[0])
    for cut in shards[1:]:
        factor_of = factor_of * one(*cut)
    return factor_of


def scatter_about(key, dims, width, limit, cuts=(), kind=jnp.bfloat16):
    entries = width * jax.random.normal(key, dims, jnp.float32)
    if cuts:
        entries = entries * block_levels(key, dims, cuts, -0.22, 0.18)
    return jnp.clip(entries, -limit, limit).astype(kind)


def setup_inputs(seed: int = 0, part: int = 0) -> dict:
    seeds = jax.random.split(jax.random.key(seed), 9)
    own_keys = jax.random.split(jax.random.fold_in(seeds[8], part), 9)
    return {
        "layer_inputs": scatter_about(own_keys[0], (TOKENS, PIPE * D), 1.0, 6.0, ((0, 4), (1, 4))),
        "labels": plant(jax.random.randint(own_keys[1], (TOKENS,), 0, 2), jax.random.fold_in(own_keys[1], 1), 0, 1).astype(jnp.int32),
        "head_weight": scatter_about(seeds[2], (D,), 1.0, 5.0, (), jnp.float32),
        "gate_up_store": scatter_about(seeds[3], (N_FSDP * CAP, N_SEGMENT, 2, BLK, BLK), (D // 2) ** -0.5, 0.125, ((0, 4), (1, 4))),
        "down_store": scatter_about(seeds[4], (N_FSDP * CAP, N_SEGMENT, BLK, BLK), (FF // 2) ** -0.5, 0.0625, ((0, 4), (1, 4))),
        "kept_rows": draw_kept_rows(jax.random.fold_in(seeds[8], 71), part),
        "owners": draw_owners(jax.random.fold_in(seeds[8], 71), part),
        "slots": draw_slots(jax.random.fold_in(seeds[8], 71), part),
    }


def forward_columns(inputs, rows, gate_up):
    tokens = inputs.shape[0]
    blocks_x = inputs.astype(jnp.float32).reshape(tokens, D // BLK, BLK)

    def one(carry, item):
        row_ids, blocks = item
        picked = blocks_x[:, row_ids, :]
        gate = jnp.einsum("mkb,kbc->mc", picked, blocks[:, 0].astype(jnp.float32), precision=lax.Precision.HIGHEST)
        up = jnp.einsum("mkb,kbc->mc", picked, blocks[:, 1].astype(jnp.float32), precision=lax.Precision.HIGHEST)
        hidden = (jax.nn.silu(gate) * up).astype(jnp.bfloat16)
        return carry, (gate, up, hidden)

    return lax.scan(one, jnp.float32(0.0), (rows, gate_up))[1]


def backward_columns(inputs, cotangent, rows, gate_up, down, gates, ups, hiddens):
    tokens = inputs.shape[0]
    blocks_x = inputs.astype(jnp.float32).reshape(tokens, D // BLK, BLK)
    blocks_d = cotangent.astype(jnp.float32).reshape(tokens, D // BLK, BLK)

    def one(carry, item):
        row_ids, blocks, down_blocks, gate, up, hidden = item
        picked = blocks_x[:, row_ids, :]
        dpicked = blocks_d[:, row_ids, :]
        dhidden = jnp.einsum("mkd,kcd->mc", dpicked, down_blocks.astype(jnp.float32), precision=lax.Precision.HIGHEST)
        sig = jax.nn.sigmoid(gate)
        dgate = (dhidden * up * sig * (1.0 + gate * (1.0 - sig))).astype(jnp.bfloat16)
        dup = (dhidden * jax.nn.silu(gate)).astype(jnp.bfloat16)
        grad_down = jnp.einsum("mc,mkd->kcd", hidden.astype(jnp.float32), dpicked, precision=lax.Precision.HIGHEST)
        grad_gate = jnp.einsum("mkb,mc->kbc", picked, dgate.astype(jnp.float32), precision=lax.Precision.HIGHEST)
        grad_up = jnp.einsum("mkb,mc->kbc", picked, dup.astype(jnp.float32), precision=lax.Precision.HIGHEST)
        spread = jnp.einsum("mc,kbc->mkb", dgate.astype(jnp.float32), blocks[:, 0].astype(jnp.float32), precision=lax.Precision.HIGHEST)
        spread = spread + jnp.einsum("mc,kbc->mkb", dup.astype(jnp.float32), blocks[:, 1].astype(jnp.float32), precision=lax.Precision.HIGHEST)
        carry = carry.at[:, row_ids, :].add(spread)
        pair_grads = jnp.stack([grad_gate, grad_up], axis=1).astype(jnp.bfloat16)
        return carry, (pair_grads, grad_down.astype(jnp.bfloat16))

    start = jnp.zeros((tokens, D // BLK, BLK), jnp.float32)
    total, grads = lax.scan(one, start, (rows, gate_up, down, gates, ups, hiddens))
    result = (cotangent.astype(jnp.float32) + total.reshape(tokens, D)).astype(jnp.bfloat16)
    return result, grads


def reference(layer_inputs, labels, head_weight, gate_up_store, down_store, kept_rows, owners, slots):
    sections = N_SEGMENT // PIPE
    ncols = FF // BLK
    tokens = layer_inputs.shape[0]
    entry = owners * CAP + slots
    column_ids = jnp.arange(ncols, dtype=jnp.int32)
    segment_ids = jnp.arange(PIPE, dtype=jnp.int32)[:, None] * sections + column_ids[None, :] // (COLS * N_FSDP)
    gate_up = gate_up_store[entry, segment_ids[:, :, None]]
    down = down_store[entry, segment_ids[:, :, None]]
    saved = []
    for segment in range(PIPE):
        inputs = layer_inputs[:, segment * D:(segment + 1) * D]
        saved.append((inputs,) + tuple(forward_columns(inputs, kept_rows[segment], gate_up[segment])))
    last = PIPE - 1
    inputs_last, gates_last, ups_last, hiddens_last = saved[last]

    def add_output(carry, item):
        row_ids, down_blocks, hidden = item
        part = jnp.einsum("mc,kcd->mkd", hidden.astype(jnp.float32), down_blocks.astype(jnp.float32), precision=lax.Precision.HIGHEST)
        return carry.at[:, row_ids, :].add(part), None

    outputs = lax.scan(add_output, jnp.zeros((tokens, D // BLK, BLK), jnp.float32), (kept_rows[last], down[last], hiddens_last))[0]
    outputs = inputs_last.astype(jnp.float32) + outputs.reshape(tokens, D)
    logits = jnp.dot(outputs, head_weight, precision=lax.Precision.HIGHEST) * (D ** -0.5)
    dlogit = jax.nn.sigmoid(logits) - labels.astype(jnp.float32)
    cotangent = (dlogit[:, None] * head_weight[None, :]).astype(jnp.bfloat16)
    gate_up_grads = jnp.zeros(gate_up_store.shape, jnp.bfloat16)
    down_grads = jnp.zeros(down_store.shape, jnp.bfloat16)
    results = [None] * PIPE
    for segment in reversed(range(PIPE)):
        inputs, gates, ups, hiddens = saved[segment]
        result, grads = backward_columns(inputs, cotangent, kept_rows[segment], gate_up[segment], down[segment], gates, ups, hiddens)
        results[segment] = result
        gate_up_grads = gate_up_grads.at[entry[segment], segment_ids[segment][:, None]].set(grads[0])
        down_grads = down_grads.at[entry[segment], segment_ids[segment][:, None]].set(grads[1])
        cotangent = result
    return jnp.concatenate(results, axis=1), gate_up_grads, down_grads
```

```python
import jax
import jax.numpy as jnp
from jax import lax
from jax.sharding import PartitionSpec as P

PIPE = 2
HI = lax.Precision.HIGHEST


def per_device(
    layer_inputs, labels, head_weight, gate_up_store, down_store, kept_rows, owners, slots
):
    members = lax.axis_size("fsdp")
    places = lax.axis_size("segment")
    sections = places // PIPE
    member = lax.axis_index("fsdp")
    place = lax.axis_index("segment")
    segment = place // sections
    section = place % sections
    is_last = segment == PIPE - 1
    tok_rows, piece_width = layer_inputs.shape
    tokens = tok_rows * members
    width = piece_width * sections
    blk = gate_up_store.shape[-1]
    capacity = gate_up_store.shape[0]
    kept = kept_rows.shape[2]
    sec_cols = kept_rows.shape[1] // sections
    nrow = width // blk
    nblocks = sec_cols * kept

    first_col = section * sec_cols
    sec_rows = lax.dynamic_slice(kept_rows, (segment, first_col, 0), (1, sec_cols, kept))
    sec_owner = lax.dynamic_slice(owners, (segment, first_col, 0), (1, sec_cols, kept))
    sec_slot = lax.dynamic_slice(slots, (segment, first_col, 0), (1, sec_cols, kept))
    sec_rows = sec_rows.reshape(nblocks)
    mine = sec_owner.reshape(nblocks) == member
    block_col = jnp.arange(nblocks, dtype=jnp.int32) // kept
    hits = mine[None, :] & (
        sec_slot.reshape(nblocks)[None, :] == jnp.arange(capacity, dtype=jnp.int32)[:, None]
    )
    valid = jnp.any(hits, axis=1)
    slot_col = jnp.sum(jnp.where(hits, block_col[None, :], 0), axis=1)
    slot_row = jnp.sum(jnp.where(hits, sec_rows[None, :], 0), axis=1)
    col_hot = valid[:, None] & (slot_col[:, None] == jnp.arange(sec_cols, dtype=jnp.int32)[None, :])
    row_hot = valid[:, None] & (slot_row[:, None] == jnp.arange(nrow, dtype=jnp.int32)[None, :])
    col_f = col_hot.astype(jnp.float32)
    col_b = col_hot.astype(jnp.bfloat16)
    row_f = row_hot.astype(jnp.float32)
    row_b = row_hot.astype(jnp.bfloat16)

    w_pair = gate_up_store[:, 0]
    w_down = down_store[:, 0]

    gathered = lax.all_gather(layer_inputs, ("fsdp", "segment"))
    gathered = gathered.reshape(members, places, tok_rows, piece_width)
    x_all = gathered.transpose(0, 2, 1, 3).reshape(tokens, places * piece_width)
    x_mine = lax.dynamic_slice_in_dim(x_all, segment * width, width, axis=1)
    x_last = x_all[:, (PIPE - 1) * width:]
    x_sel = jnp.einsum("cr,trb->ctb", row_b, x_mine.reshape(tokens, nrow, blk))
    x_sel = x_sel.astype(jnp.bfloat16)

    gu_slot = jnp.einsum("cta,cgab->ctgb", x_sel, w_pair, preferred_element_type=jnp.float32)
    gu_part = jnp.einsum("cj,ctgb->gtjb", col_f, gu_slot, precision=HI)
    head_rows = head_weight.reshape(nrow, blk)
    head_sel = jnp.einsum("cr,rd->cd", row_f, head_rows, precision=HI)
    folded = jnp.einsum(
        "chd,cd->ch", w_down.astype(jnp.float32), head_sel, precision=HI
    )
    f_part = jnp.einsum("cj,ch->jh", col_f, folded, precision=HI)
    packed = jnp.concatenate(
        [gu_part.reshape(2 * tokens, sec_cols, blk), f_part[None]], axis=0
    )
    packed = lax.psum(packed, "fsdp")
    gate = packed[:tokens]
    up = packed[tokens:2 * tokens]
    f_sum = packed[2 * tokens]
    sig = jax.nn.sigmoid(gate)
    hidden = (gate * sig * up).astype(jnp.bfloat16)

    branch = jnp.einsum("tjh,jh->t", hidden.astype(jnp.float32), f_sum, precision=HI)
    branch = jnp.where(is_last, branch, 0.0)
    branch = lax.psum(branch, "segment")
    x_term = jnp.einsum("td,d->t", x_last.astype(jnp.float32), head_weight, precision=HI)
    logits = (x_term + branch) * width ** (-0.5)
    dlogit = jax.nn.sigmoid(logits) - labels.astype(jnp.float32)
    dout_last = (dlogit[:, None] * head_weight[None, :]).astype(jnp.bfloat16)

    def gate_grads(dhidden):
        dgate = (dhidden * up * sig * (1.0 + gate * (1.0 - sig))).astype(jnp.bfloat16)
        dup = (dhidden * gate * sig).astype(jnp.bfloat16)
        pair = jnp.stack([dgate, dup], axis=2)
        return jnp.einsum("cj,tjgb->ctgb", col_b, pair).astype(jnp.bfloat16)

    def spread_rows(d_sel):
        spread = jnp.einsum(
            "ctgb,cgab->cta", d_sel, w_pair, preferred_element_type=jnp.float32
        )
        return jnp.einsum("cr,cta->tra", row_f, spread, precision=HI).reshape(tokens, width)

    d_sel_last = gate_grads(dlogit[:, None, None] * f_sum[None])
    part_last = jnp.where(is_last, spread_rows(d_sel_last), 0.0)
    sum_last = lax.psum(part_last, ("fsdp", "segment"))
    grad_last = (dout_last.astype(jnp.float32) + sum_last).astype(jnp.bfloat16)

    dout_sel = jnp.einsum("cr,trd->ctd", row_b, grad_last.reshape(tokens, nrow, blk))
    dout_sel = dout_sel.astype(jnp.bfloat16)
    dh_slot = jnp.einsum("ctd,chd->cth", dout_sel, w_down, preferred_element_type=jnp.float32)
    dh_part = jnp.einsum("cj,cth->tjh", col_f, dh_slot, precision=HI)
    dhidden_first = lax.psum(dh_part, "fsdp")
    d_sel_first = gate_grads(dhidden_first)
    part_first = jnp.where(is_last, 0.0, spread_rows(d_sel_first))
    sum_first = lax.psum(part_first, ("fsdp", "segment"))
    grad_first = (grad_last.astype(jnp.float32) + sum_first).astype(jnp.bfloat16)

    rows_at = member * tok_rows
    cols_at = section * piece_width
    grads = jnp.where(is_last, grad_last, grad_first)
    input_grads = lax.dynamic_slice(grads, (rows_at, cols_at), (tok_rows, piece_width))

    d_sel = jnp.where(is_last, d_sel_last, d_sel_first)
    cot_sel = jnp.where(
        is_last,
        jnp.einsum("cr,trd->ctd", row_b, dout_last.reshape(tokens, nrow, blk)).astype(
            jnp.bfloat16
        ),
        dout_sel,
    )
    hid_sel = jnp.einsum("cj,tjh->cth", col_b, hidden).astype(jnp.bfloat16)
    grad_pair = jnp.einsum(
        "cta,ctgb->cgab", x_sel, d_sel, preferred_element_type=jnp.float32
    ).astype(jnp.bfloat16)
    grad_down = jnp.einsum(
        "cth,ctd->chd", hid_sel, cot_sel, preferred_element_type=jnp.float32
    ).astype(jnp.bfloat16)
    zero_bf = jnp.zeros((), jnp.bfloat16)
    grad_pair = jnp.where(valid[:, None, None, None], grad_pair, zero_bf)
    grad_down = jnp.where(valid[:, None, None], grad_down, zero_bf)
    return (input_grads, grad_pair[:, None], grad_down[:, None])


def solution(mesh):
    return jax.shard_map(
        per_device,
        mesh=mesh,
        in_specs=(
            P(("groups", "fsdp"), "segment"),
            P("groups"),
            P(),
            P("fsdp", "segment", None, None, None),
            P("fsdp", "segment", None, None),
            P(),
            P(),
            P(),
        ),
        out_specs=(
            P(("groups", "fsdp"), "segment"),
            P(("groups", "fsdp"), "segment", None, None, None),
            P(("groups", "fsdp"), "segment", None, None),
        ),
        check_vma=False,
    )
```

```python
import jax
import jax.numpy as jnp
from jax import lax
from jax.sharding import PartitionSpec as P

PIPE = 2
HI = lax.Precision.HIGHEST


def bits_of(size):
    return size.bit_length() - 1


def swapped(x, axis, bit):
    size = lax.axis_size(axis)
    return lax.ppermute(x, axis, [(i, i ^ (1 << bit)) for i in range(size)])


def all_sum(x, axis, levels):
    for bit in range(levels):
        x = x + swapped(x, axis, bit)
    return x


def gather_along(x, axis, index, levels, dim):
    for bit in range(levels):
        other = swapped(x, axis, bit)
        upper = (index >> bit) & 1 == 1
        x = jnp.where(
            upper,
            jnp.concatenate([other, x], axis=dim),
            jnp.concatenate([x, other], axis=dim),
        )
    return x


def scatter_along(x, axis, index, levels, dim):
    for bit in reversed(range(levels)):
        half = x.shape[dim] // 2
        upper = (index >> bit) & 1
        keep = lax.dynamic_slice_in_dim(x, upper * half, half, axis=dim)
        send = lax.dynamic_slice_in_dim(x, (1 - upper) * half, half, axis=dim)
        x = keep + swapped(send, axis, bit)
    return x


def per_device(
    layer_inputs, labels, head_weight, gate_up_store, down_store, kept_rows, owners, slots
):
    members = lax.axis_size("fsdp")
    places = lax.axis_size("segment")
    sections = places // PIPE
    member = lax.axis_index("fsdp")
    place = lax.axis_index("segment")
    segment = place // sections
    section = place % sections
    is_last = segment == PIPE - 1
    tok_rows, piece_width = layer_inputs.shape
    tokens = tok_rows * members
    width = piece_width * sections
    blk = gate_up_store.shape[-1]
    capacity = gate_up_store.shape[0]
    kept = kept_rows.shape[2]
    sec_cols = kept_rows.shape[1] // sections
    nrow = width // blk
    nblocks = sec_cols * kept

    first_col = section * sec_cols
    sec_rows = lax.dynamic_slice(kept_rows, (segment, first_col, 0), (1, sec_cols, kept))
    sec_owner = lax.dynamic_slice(owners, (segment, first_col, 0), (1, sec_cols, kept))
    sec_slot = lax.dynamic_slice(slots, (segment, first_col, 0), (1, sec_cols, kept))
    sec_rows = sec_rows.reshape(nblocks)
    mine = sec_owner.reshape(nblocks) == member
    block_col = jnp.arange(nblocks, dtype=jnp.int32) // kept
    hits = mine[None, :] & (
        sec_slot.reshape(nblocks)[None, :] == jnp.arange(capacity, dtype=jnp.int32)[:, None]
    )
    valid = jnp.any(hits, axis=1)
    slot_col = jnp.sum(jnp.where(hits, block_col[None, :], 0), axis=1)
    slot_row = jnp.sum(jnp.where(hits, sec_rows[None, :], 0), axis=1)
    col_hot = valid[:, None] & (slot_col[:, None] == jnp.arange(sec_cols, dtype=jnp.int32)[None, :])
    row_hot = valid[:, None] & (slot_row[:, None] == jnp.arange(nrow, dtype=jnp.int32)[None, :])
    col_f = col_hot.astype(jnp.float32)
    col_b = col_hot.astype(jnp.bfloat16)
    row_f = row_hot.astype(jnp.float32)
    row_b = row_hot.astype(jnp.bfloat16)

    w_pair = gate_up_store[:, 0]
    w_down = down_store[:, 0]

    fsdp_bits = bits_of(members)
    sec_bits = bits_of(sections)

    x_mine = gather_along(layer_inputs, "segment", section, sec_bits, 1)
    x_mine = gather_along(x_mine, "fsdp", member, fsdp_bits, 0)
    x_sel = jnp.einsum("cr,trb->ctb", row_b, x_mine.reshape(tokens, nrow, blk))
    x_sel = x_sel.astype(jnp.bfloat16)

    gu_slot = jnp.einsum("cta,cgab->ctgb", x_sel, w_pair, preferred_element_type=jnp.float32)
    gu_part = jnp.einsum("cj,ctgb->gtjb", col_f, gu_slot, precision=HI)
    head_rows = head_weight.reshape(nrow, blk)
    head_sel = jnp.einsum("cr,rd->cd", row_f, head_rows, precision=HI)
    head_hi = head_sel.astype(jnp.bfloat16)
    head_lo = (head_sel - head_hi.astype(jnp.float32)).astype(jnp.bfloat16)
    head_two = jnp.stack([head_hi, head_lo], axis=1)
    folded = jnp.einsum(
        "chd,ckd->chk", w_down, head_two, preferred_element_type=jnp.float32
    ).sum(axis=2)
    f_part = jnp.einsum("cj,ch->jh", col_f, folded, precision=HI)
    packed = jnp.concatenate(
        [gu_part.reshape(2 * tokens, sec_cols, blk), f_part[None]], axis=0
    )
    packed = all_sum(packed, "fsdp", fsdp_bits)
    gate = packed[:tokens]
    up = packed[tokens:2 * tokens]
    f_sum = packed[2 * tokens]
    sig = jax.nn.sigmoid(gate)
    hidden = (gate * sig * up).astype(jnp.bfloat16)

    branch = jnp.einsum("tjh,jh->t", hidden.astype(jnp.float32), f_sum, precision=HI)
    x_term = jnp.einsum("td,d->t", x_mine.astype(jnp.float32), head_weight, precision=HI)
    branch = branch + jnp.where(section == 0, x_term, 0.0)
    logits = all_sum(branch, "segment", sec_bits) * width ** (-0.5)
    dlogit = jax.nn.sigmoid(logits) - labels.astype(jnp.float32)
    dout_last = (dlogit[:, None] * head_weight[None, :]).astype(jnp.bfloat16)

    def gate_grads(dhidden):
        dgate = (dhidden * up * sig * (1.0 + gate * (1.0 - sig))).astype(jnp.bfloat16)
        dup = (dhidden * gate * sig).astype(jnp.bfloat16)
        pair = jnp.stack([dgate, dup], axis=2)
        return jnp.einsum("cj,tjgb->ctgb", col_b, pair).astype(jnp.bfloat16)

    def spread_rows(d_sel):
        spread = jnp.einsum(
            "ctgb,cgab->cta", d_sel, w_pair, preferred_element_type=jnp.float32
        )
        return jnp.einsum("cr,cta->tra", row_f, spread, precision=HI).reshape(tokens, width)

    d_sel_last = gate_grads(dlogit[:, None, None] * f_sum[None])
    sum_last = all_sum(spread_rows(d_sel_last), "fsdp", fsdp_bits)
    sum_last = all_sum(sum_last, "segment", sec_bits)
    grad_last = (dout_last.astype(jnp.float32) + sum_last).astype(jnp.bfloat16)
    handed = lax.ppermute(
        grad_last, "segment", [(i, i - sections) for i in range(sections, places)]
    )
    dout_first = jnp.where(is_last, grad_last, handed)

    dout_sel = jnp.einsum("cr,trd->ctd", row_b, dout_first.reshape(tokens, nrow, blk))
    dout_sel = dout_sel.astype(jnp.bfloat16)
    dh_slot = jnp.einsum("ctd,chd->cth", dout_sel, w_down, preferred_element_type=jnp.float32)
    dh_part = jnp.einsum("cj,cth->tjh", col_f, dh_slot, precision=HI)
    dhidden_first = all_sum(dh_part, "fsdp", fsdp_bits)
    d_sel_first = gate_grads(dhidden_first)
    part_first = spread_rows(d_sel_first)
    part_first = scatter_along(part_first, "fsdp", member, fsdp_bits, 0)
    part_first = scatter_along(part_first, "segment", section, sec_bits, 1)

    rows_at = member * tok_rows
    cols_at = section * piece_width
    own_last = lax.dynamic_slice(grad_last, (rows_at, cols_at), (tok_rows, piece_width))
    own_dout = lax.dynamic_slice(dout_first, (rows_at, cols_at), (tok_rows, piece_width))
    grad_first = (own_dout.astype(jnp.float32) + part_first).astype(jnp.bfloat16)
    input_grads = jnp.where(is_last, own_last, grad_first)

    d_sel = jnp.where(is_last, d_sel_last, d_sel_first)
    cot_sel = jnp.where(
        is_last,
        jnp.einsum("cr,trd->ctd", row_b, dout_last.reshape(tokens, nrow, blk)).astype(
            jnp.bfloat16
        ),
        dout_sel,
    )
    hid_sel = jnp.einsum("cj,tjh->cth", col_b, hidden).astype(jnp.bfloat16)
    x_pair = jnp.broadcast_to(x_sel[:, None], (capacity, 2, tokens, blk))
    grad_pair = jnp.einsum(
        "cgta,cgtb->cgab", x_pair, d_sel.transpose(0, 2, 1, 3),
        preferred_element_type=jnp.float32,
    ).astype(jnp.bfloat16)
    grad_down = jnp.einsum(
        "cth,ctd->chd", hid_sel, cot_sel, preferred_element_type=jnp.float32
    ).astype(jnp.bfloat16)
    zero_bf = jnp.zeros((), jnp.bfloat16)
    grad_pair = jnp.where(valid[:, None, None, None], grad_pair, zero_bf)
    grad_down = jnp.where(valid[:, None, None], grad_down, zero_bf)
    return (input_grads, grad_pair[:, None], grad_down[:, None])


def solution(mesh):
    return jax.shard_map(
        per_device,
        mesh=mesh,
        in_specs=(
            P(("groups", "fsdp"), "segment"),
            P("groups"),
            P(),
            P("fsdp", "segment", None, None, None),
            P("fsdp", "segment", None, None),
            P(),
            P(),
            P(),
        ),
        out_specs=(
            P(("groups", "fsdp"), "segment"),
            P(("groups", "fsdp"), "segment", None, None, None),
            P(("groups", "fsdp"), "segment", None, None),
        ),
        check_vma=False,
    )
```

```python
import jax
import jax.numpy as jnp
from jax import lax
from jax.sharding import PartitionSpec as P

PIPE = 2
HI = lax.Precision.HIGHEST


def bits_of(size):
    return size.bit_length() - 1


def swapped(x, axis, bit):
    size = lax.axis_size(axis)
    return lax.ppermute(x, axis, [(i, i ^ (1 << bit)) for i in range(size)])


def all_sum(x, axis, levels):
    for bit in range(levels):
        x = x + swapped(x, axis, bit)
    return x


def gather_along(x, axis, index, levels, dim):
    for bit in range(levels):
        other = swapped(x, axis, bit)
        upper = (index >> bit) & 1 == 1
        x = jnp.where(
            upper,
            jnp.concatenate([other, x], axis=dim),
            jnp.concatenate([x, other], axis=dim),
        )
    return x


def scatter_along(x, axis, index, levels, dim):
    for bit in reversed(range(levels)):
        half = x.shape[dim] // 2
        upper = (index >> bit) & 1
        keep = lax.dynamic_slice_in_dim(x, upper * half, half, axis=dim)
        send = lax.dynamic_slice_in_dim(x, (1 - upper) * half, half, axis=dim)
        x = keep + swapped(send, axis, bit)
    return x


def scatter_blocks(x, axis, index, levels):
    x = x.reshape((2,) * levels + x.shape[1:])
    for bit in range(levels):
        pos = levels - 1 - bit
        mine = (index >> bit) & 1
        keep = lax.dynamic_index_in_dim(x, mine, pos, keepdims=False)
        send = lax.dynamic_index_in_dim(x, 1 - mine, pos, keepdims=False)
        x = keep + swapped(send, axis, bit)
    return x


def gather_blocks(x, axis, index, levels):
    for count, bit in enumerate(reversed(range(levels))):
        other = swapped(x, axis, bit)
        upper = (index >> bit) & 1 == 1
        x = jnp.where(
            upper, jnp.stack([other, x], axis=count), jnp.stack([x, other], axis=count)
        )
    return x.reshape((-1,) + x.shape[levels:])


def per_device(
    layer_inputs, labels, head_weight, gate_up_store, down_store, kept_rows, owners, slots
):
    members = lax.axis_size("fsdp")
    places = lax.axis_size("segment")
    sections = places // PIPE
    member = lax.axis_index("fsdp")
    place = lax.axis_index("segment")
    segment = place // sections
    section = place % sections
    is_last = segment == PIPE - 1
    tok_rows, piece_width = layer_inputs.shape
    tokens = tok_rows * members
    width = piece_width * sections
    blk = gate_up_store.shape[-1]
    capacity = gate_up_store.shape[0]
    kept = kept_rows.shape[2]
    sec_cols = kept_rows.shape[1] // sections
    nrow = width // blk
    nblocks = sec_cols * kept

    first_col = section * sec_cols
    sec_rows = lax.dynamic_slice(kept_rows, (segment, first_col, 0), (1, sec_cols, kept))
    sec_owner = lax.dynamic_slice(owners, (segment, first_col, 0), (1, sec_cols, kept))
    sec_slot = lax.dynamic_slice(slots, (segment, first_col, 0), (1, sec_cols, kept))
    sec_rows = sec_rows.reshape(nblocks)
    mine = sec_owner.reshape(nblocks) == member
    block_col = jnp.arange(nblocks, dtype=jnp.int32) // kept
    hits = mine[None, :] & (
        sec_slot.reshape(nblocks)[None, :] == jnp.arange(capacity, dtype=jnp.int32)[:, None]
    )
    valid = jnp.any(hits, axis=1)
    slot_col = jnp.sum(jnp.where(hits, block_col[None, :], 0), axis=1)
    slot_row = jnp.sum(jnp.where(hits, sec_rows[None, :], 0), axis=1)
    col_hot = valid[:, None] & (slot_col[:, None] == jnp.arange(sec_cols, dtype=jnp.int32)[None, :])
    row_hot = valid[:, None] & (slot_row[:, None] == jnp.arange(nrow, dtype=jnp.int32)[None, :])
    col_f = col_hot.astype(jnp.float32)
    col_b = col_hot.astype(jnp.bfloat16)
    row_f = row_hot.astype(jnp.float32)
    row_b = row_hot.astype(jnp.bfloat16)

    w_pair = gate_up_store[:, 0]
    w_down = down_store[:, 0]

    fsdp_bits = bits_of(members)
    sec_bits = bits_of(sections)

    x_mine = gather_along(layer_inputs, "segment", section, sec_bits, 1)
    x_mine = gather_along(x_mine, "fsdp", member, fsdp_bits, 0)
    x_sel = jnp.einsum("cr,trb->ctb", row_b, x_mine.reshape(tokens, nrow, blk))
    x_sel = x_sel.astype(jnp.bfloat16)

    gu_slot = jnp.einsum("cta,cgab->ctgb", x_sel, w_pair, preferred_element_type=jnp.float32)
    gu_part = jnp.einsum("cj,ctgb->gtjb", col_f, gu_slot, precision=HI)
    head_rows = head_weight.reshape(nrow, blk)
    head_sel = jnp.einsum("cr,rd->cd", row_f, head_rows, precision=HI)
    head_hi = head_sel.astype(jnp.bfloat16)
    head_lo = (head_sel - head_hi.astype(jnp.float32)).astype(jnp.bfloat16)
    head_two = jnp.stack([head_hi, head_lo], axis=1)
    folded = jnp.einsum(
        "chd,ckd->chk", w_down, head_two, preferred_element_type=jnp.float32
    ).sum(axis=2)
    f_part = jnp.einsum("cj,ch->jh", col_f, folded, precision=HI)
    cols_per = sec_cols // members
    packed = jnp.concatenate(
        [gu_part.reshape(2 * tokens, sec_cols, blk), f_part[None]], axis=0
    )
    packed = packed.reshape(2 * tokens + 1, members, cols_per, blk).transpose(1, 0, 2, 3)
    packed = scatter_blocks(packed, "fsdp", member, fsdp_bits)
    gate = packed[:tokens]
    up = packed[tokens:2 * tokens]
    f_sum = packed[2 * tokens]
    sig = jax.nn.sigmoid(gate)
    hidden_own = (gate * sig * up).astype(jnp.bfloat16)

    branch = jnp.einsum("tjh,jh->t", hidden_own.astype(jnp.float32), f_sum, precision=HI)
    x_term = jnp.einsum("td,d->t", x_mine.astype(jnp.float32), head_weight, precision=HI)
    branch = branch + jnp.where((section == 0) & (member == 0), x_term, 0.0)
    logits = all_sum(branch, "fsdp", fsdp_bits)
    logits = all_sum(logits, "segment", sec_bits) * width ** (-0.5)
    dlogit = jax.nn.sigmoid(logits) - labels.astype(jnp.float32)
    dout_last = (dlogit[:, None] * head_weight[None, :]).astype(jnp.bfloat16)

    def gate_grads(dhidden):
        dgate = (dhidden * up * sig * (1.0 + gate * (1.0 - sig))).astype(jnp.bfloat16)
        dup = (dhidden * gate * sig).astype(jnp.bfloat16)
        return dgate, dup

    def share(parts):
        whole = gather_blocks(jnp.stack(parts), "fsdp", member, fsdp_bits)
        n = len(parts)
        return whole.transpose(1, 2, 0, 3, 4).reshape(n, tokens, sec_cols, blk)

    def select_pair(dgate, dup):
        pair = jnp.stack([dgate, dup], axis=2)
        return jnp.einsum("cj,tjgb->ctgb", col_b, pair).astype(jnp.bfloat16)

    def spread_rows(d_sel):
        spread = jnp.einsum(
            "ctgb,cgab->cta", d_sel, w_pair, preferred_element_type=jnp.float32
        )
        return jnp.einsum("cr,cta->tra", row_f, spread, precision=HI).reshape(tokens, width)

    dgate_last, dup_last = gate_grads(dlogit[:, None, None] * f_sum[None])
    shared = share([hidden_own, dgate_last, dup_last])
    hidden = shared[0]
    d_sel_last = select_pair(shared[1], shared[2])
    sum_last = all_sum(spread_rows(d_sel_last), "fsdp", fsdp_bits)
    sum_last = all_sum(sum_last, "segment", sec_bits)
    grad_last = (dout_last.astype(jnp.float32) + sum_last).astype(jnp.bfloat16)
    handed = lax.ppermute(
        grad_last, "segment", [(i, i - sections) for i in range(sections, places)]
    )
    dout_first = jnp.where(is_last, grad_last, handed)

    dout_sel = jnp.einsum("cr,trd->ctd", row_b, dout_first.reshape(tokens, nrow, blk))
    dout_sel = dout_sel.astype(jnp.bfloat16)
    dh_slot = jnp.einsum("ctd,chd->cth", dout_sel, w_down, preferred_element_type=jnp.float32)
    dh_part = jnp.einsum("cj,cth->tjh", col_f, dh_slot, precision=HI)
    dh_part = dh_part.reshape(tokens, members, cols_per, blk).transpose(1, 0, 2, 3)
    dhidden_first = scatter_blocks(dh_part, "fsdp", member, fsdp_bits)
    dgate_first, dup_first = gate_grads(dhidden_first)
    shared_first = share([dgate_first, dup_first])
    d_sel_first = select_pair(shared_first[0], shared_first[1])
    part_first = spread_rows(d_sel_first)
    part_first = scatter_along(part_first, "fsdp", member, fsdp_bits, 0)
    part_first = scatter_along(part_first, "segment", section, sec_bits, 1)

    rows_at = member * tok_rows
    cols_at = section * piece_width
    own_last = lax.dynamic_slice(grad_last, (rows_at, cols_at), (tok_rows, piece_width))
    own_dout = lax.dynamic_slice(dout_first, (rows_at, cols_at), (tok_rows, piece_width))
    grad_first = (own_dout.astype(jnp.float32) + part_first).astype(jnp.bfloat16)
    input_grads = jnp.where(is_last, own_last, grad_first)

    d_sel = jnp.where(is_last, d_sel_last, d_sel_first)
    cot_sel = jnp.where(
        is_last,
        jnp.einsum("cr,trd->ctd", row_b, dout_last.reshape(tokens, nrow, blk)).astype(
            jnp.bfloat16
        ),
        dout_sel,
    )
    hid_sel = jnp.einsum("cj,tjh->cth", col_b, hidden).astype(jnp.bfloat16)
    x_pair = jnp.broadcast_to(x_sel[:, None], (capacity, 2, tokens, blk))
    grad_pair = jnp.einsum(
        "cgta,cgtb->cgab", x_pair, d_sel.transpose(0, 2, 1, 3),
        preferred_element_type=jnp.float32,
    ).astype(jnp.bfloat16)
    grad_down = jnp.einsum(
        "cth,ctd->chd", hid_sel, cot_sel, preferred_element_type=jnp.float32
    ).astype(jnp.bfloat16)
    zero_bf = jnp.zeros((), jnp.bfloat16)
    grad_pair = jnp.where(valid[:, None, None, None], grad_pair, zero_bf)
    grad_down = jnp.where(valid[:, None, None], grad_down, zero_bf)
    return (input_grads, grad_pair[:, None], grad_down[:, None])


def solution(mesh):
    return jax.shard_map(
        per_device,
        mesh=mesh,
        in_specs=(
            P(("groups", "fsdp"), "segment"),
            P("groups"),
            P(),
            P("fsdp", "segment", None, None, None),
            P("fsdp", "segment", None, None),
            P(),
            P(),
            P(),
        ),
        out_specs=(
            P(("groups", "fsdp"), "segment"),
            P(("groups", "fsdp"), "segment", None, None, None),
            P(("groups", "fsdp"), "segment", None, None),
        ),
        check_vma=False,
    )
```

```python
import jax
import jax.numpy as jnp
from jax import lax
from jax.sharding import PartitionSpec as P

PIPE = 2
HI = lax.Precision.HIGHEST
HOT = lax.Precision.HIGH


def bits_of(size):
    return size.bit_length() - 1


def swapped(x, axis, bit):
    size = lax.axis_size(axis)
    return lax.ppermute(x, axis, [(i, i ^ (1 << bit)) for i in range(size)])


def all_sum(x, axis, levels):
    for bit in range(levels):
        x = x + swapped(x, axis, bit)
    return x


def gather_along(x, axis, index, levels, dim):
    for bit in range(levels):
        other = swapped(x, axis, bit)
        upper = (index >> bit) & 1 == 1
        x = jnp.where(
            upper,
            jnp.concatenate([other, x], axis=dim),
            jnp.concatenate([x, other], axis=dim),
        )
    return x


def scatter_along(x, axis, index, levels, dim):
    for bit in reversed(range(levels)):
        half = x.shape[dim] // 2
        upper = (index >> bit) & 1
        keep = lax.dynamic_slice_in_dim(x, upper * half, half, axis=dim)
        send = lax.dynamic_slice_in_dim(x, (1 - upper) * half, half, axis=dim)
        x = keep + swapped(send, axis, bit)
    return x


def scatter_blocks(x, axis, index, levels):
    x = x.reshape((2,) * levels + x.shape[1:])
    for bit in range(levels):
        pos = levels - 1 - bit
        mine = (index >> bit) & 1
        keep = lax.dynamic_index_in_dim(x, mine, pos, keepdims=False)
        send = lax.dynamic_index_in_dim(x, 1 - mine, pos, keepdims=False)
        x = keep + swapped(send, axis, bit)
    return x


def gather_blocks(x, axis, index, levels):
    for count, bit in enumerate(reversed(range(levels))):
        other = swapped(x, axis, bit)
        upper = (index >> bit) & 1 == 1
        x = jnp.where(
            upper, jnp.stack([other, x], axis=count), jnp.stack([x, other], axis=count)
        )
    return x.reshape((-1,) + x.shape[levels:])


def per_device(
    layer_inputs, labels, head_weight, gate_up_store, down_store, kept_rows, owners, slots
):
    members = lax.axis_size("fsdp")
    places = lax.axis_size("segment")
    sections = places // PIPE
    member = lax.axis_index("fsdp")
    place = lax.axis_index("segment")
    segment = place // sections
    section = place % sections
    is_last = segment == PIPE - 1
    tok_rows, piece_width = layer_inputs.shape
    tokens = tok_rows * members
    width = piece_width * sections
    blk = gate_up_store.shape[-1]
    capacity = gate_up_store.shape[0]
    kept = kept_rows.shape[2]
    sec_cols = kept_rows.shape[1] // sections
    nrow = width // blk
    nblocks = sec_cols * kept

    first_col = section * sec_cols
    sec_rows = lax.dynamic_slice(kept_rows, (segment, first_col, 0), (1, sec_cols, kept))
    sec_owner = lax.dynamic_slice(owners, (segment, first_col, 0), (1, sec_cols, kept))
    sec_slot = lax.dynamic_slice(slots, (segment, first_col, 0), (1, sec_cols, kept))
    sec_rows = sec_rows.reshape(nblocks)
    mine = sec_owner.reshape(nblocks) == member
    block_col = jnp.arange(nblocks, dtype=jnp.int32) // kept
    hits = mine[None, :] & (
        sec_slot.reshape(nblocks)[None, :] == jnp.arange(capacity, dtype=jnp.int32)[:, None]
    )
    valid = jnp.any(hits, axis=1)
    slot_col = jnp.sum(jnp.where(hits, block_col[None, :], 0), axis=1)
    slot_row = jnp.sum(jnp.where(hits, sec_rows[None, :], 0), axis=1)
    col_hot = valid[:, None] & (slot_col[:, None] == jnp.arange(sec_cols, dtype=jnp.int32)[None, :])
    row_hot = valid[:, None] & (slot_row[:, None] == jnp.arange(nrow, dtype=jnp.int32)[None, :])
    col_f = col_hot.astype(jnp.float32)
    col_b = col_hot.astype(jnp.bfloat16)
    row_f = row_hot.astype(jnp.float32)
    row_b = row_hot.astype(jnp.bfloat16)

    w_pair = gate_up_store[:, 0]
    w_down = down_store[:, 0]

    fsdp_bits = bits_of(members)
    sec_bits = bits_of(sections)

    x_mine = gather_along(layer_inputs, "segment", section, sec_bits, 1)
    x_mine = gather_along(x_mine, "fsdp", member, fsdp_bits, 0)
    x_sel = jnp.einsum("cr,trb->ctb", row_b, x_mine.reshape(tokens, nrow, blk))
    x_sel = x_sel.astype(jnp.bfloat16)

    gu_slot = jnp.einsum("cta,cgab->ctgb", x_sel, w_pair, preferred_element_type=jnp.float32)
    gu_part = jnp.einsum("cj,ctgb->gtjb", col_f, gu_slot, precision=HOT)
    head_rows = head_weight.reshape(nrow, blk)
    head_sel = jnp.einsum("cr,rd->cd", row_f, head_rows, precision=HI)
    head_hi = head_sel.astype(jnp.bfloat16)
    head_lo = (head_sel - head_hi.astype(jnp.float32)).astype(jnp.bfloat16)
    head_two = jnp.stack([head_hi, head_lo], axis=1)
    folded = jnp.einsum(
        "chd,ckd->chk", w_down, head_two, preferred_element_type=jnp.float32
    ).sum(axis=2)
    f_part = jnp.einsum("cj,ch->jh", col_f, folded, precision=HOT)
    cols_per = sec_cols // members
    packed = gu_part.reshape(2 * tokens, members, cols_per, blk).transpose(1, 0, 2, 3)
    packed = scatter_blocks(packed, "fsdp", member, fsdp_bits)
    gate = packed[:tokens]
    up = packed[tokens:]
    f_sum = scatter_blocks(f_part.reshape(members, cols_per, blk), "fsdp", member, fsdp_bits)
    sig = jax.nn.sigmoid(gate)
    hidden_own = (gate * sig * up).astype(jnp.bfloat16)

    branch = jnp.einsum("tjh,jh->t", hidden_own.astype(jnp.float32), f_sum, precision=HI)
    x_term = jnp.einsum("td,d->t", x_mine.astype(jnp.float32), head_weight, precision=HI)
    branch = branch + jnp.where((section == 0) & (member == 0), x_term, 0.0)
    logits = all_sum(branch, "fsdp", fsdp_bits)
    logits = all_sum(logits, "segment", sec_bits) * width ** (-0.5)
    dlogit = jax.nn.sigmoid(logits) - labels.astype(jnp.float32)
    dout_last = (dlogit[:, None] * head_weight[None, :]).astype(jnp.bfloat16)

    def gate_grads(dhidden):
        dgate = (dhidden * up * sig * (1.0 + gate * (1.0 - sig))).astype(jnp.bfloat16)
        dup = (dhidden * gate * sig).astype(jnp.bfloat16)
        return dgate, dup

    def share(parts):
        whole = gather_blocks(jnp.stack(parts), "fsdp", member, fsdp_bits)
        n = len(parts)
        return whole.transpose(1, 2, 0, 3, 4).reshape(n, tokens, sec_cols, blk)

    def select_pair(dgate, dup):
        pair = jnp.stack([dgate, dup], axis=2)
        return jnp.einsum("cj,tjgb->ctgb", col_b, pair).astype(jnp.bfloat16)

    def spread_rows(d_sel):
        spread = jnp.einsum(
            "ctgb,cgab->cta", d_sel, w_pair, preferred_element_type=jnp.float32
        )
        return jnp.einsum("cr,cta->tra", row_f, spread, precision=HOT).reshape(tokens, width)

    dgate_last, dup_last = gate_grads(dlogit[:, None, None] * f_sum[None])
    shared = share([hidden_own, dgate_last, dup_last])
    hidden = shared[0]
    d_sel_last = select_pair(shared[1], shared[2])
    part_last = spread_rows(d_sel_last).reshape(members, tok_rows, width)
    rows_last = scatter_blocks(part_last, "fsdp", member, fsdp_bits)
    rows_last = all_sum(rows_last, "segment", sec_bits)
    rows_at = member * tok_rows
    cols_at = section * piece_width
    dout_rows = lax.dynamic_slice_in_dim(dout_last, rows_at, tok_rows, axis=0)
    grad_last = (dout_rows.astype(jnp.float32) + rows_last).astype(jnp.bfloat16)
    handed = lax.ppermute(
        grad_last, "segment", [(i, i - sections) for i in range(sections, places)]
    )
    first_rows = jnp.where(is_last, grad_last, handed)
    dout_first = gather_blocks(first_rows, "fsdp", member, fsdp_bits).reshape(tokens, width)

    dout_sel = jnp.einsum("cr,trd->ctd", row_b, dout_first.reshape(tokens, nrow, blk))
    dout_sel = dout_sel.astype(jnp.bfloat16)
    dh_slot = jnp.einsum("ctd,chd->cth", dout_sel, w_down, preferred_element_type=jnp.float32)
    dh_part = jnp.einsum("cj,cth->tjh", col_f, dh_slot, precision=HOT)
    dh_part = dh_part.reshape(tokens, members, cols_per, blk).transpose(1, 0, 2, 3)
    dhidden_first = scatter_blocks(dh_part, "fsdp", member, fsdp_bits)
    dgate_first, dup_first = gate_grads(dhidden_first)
    shared_first = share([dgate_first, dup_first])
    cot_sel = jnp.where(
        is_last,
        jnp.einsum("cr,trd->ctd", row_b, dout_last.reshape(tokens, nrow, blk)).astype(
            jnp.bfloat16
        ),
        dout_sel,
    )
    hid_sel = jnp.einsum("cj,tjh->cth", col_b, hidden).astype(jnp.bfloat16)
    grad_down = jnp.einsum(
        "cth,ctd->chd", hid_sel, cot_sel, preferred_element_type=jnp.float32
    ).astype(jnp.bfloat16)
    zero_bf = jnp.zeros((), jnp.bfloat16)
    grad_down = jnp.where(valid[:, None, None], grad_down, zero_bf)
    grad_down, shared_first = lax.optimization_barrier((grad_down, shared_first))
    d_sel_first = select_pair(shared_first[0], shared_first[1])
    part_first = spread_rows(d_sel_first).reshape(members, tok_rows, width)
    part_first = scatter_blocks(part_first, "fsdp", member, fsdp_bits)
    part_first = part_first.reshape(tok_rows, sections, piece_width).transpose(1, 0, 2)
    part_first = scatter_blocks(part_first, "segment", section, sec_bits)

    own_last = lax.dynamic_slice_in_dim(grad_last, cols_at, piece_width, axis=1)
    own_dout = lax.dynamic_slice(dout_first, (rows_at, cols_at), (tok_rows, piece_width))
    grad_first = (own_dout.astype(jnp.float32) + part_first).astype(jnp.bfloat16)
    input_grads = jnp.where(is_last, own_last, grad_first)

    d_sel = jnp.where(is_last, d_sel_last, d_sel_first)
    x_pair = jnp.broadcast_to(x_sel[:, None], (capacity, 2, tokens, blk))
    grad_pair = jnp.einsum(
        "cgta,cgtb->cgab", x_pair, d_sel.transpose(0, 2, 1, 3),
        preferred_element_type=jnp.float32,
    ).astype(jnp.bfloat16)
    grad_pair = jnp.where(valid[:, None, None, None], grad_pair, zero_bf)
    return (input_grads, grad_pair[:, None], grad_down[:, None])


def solution(mesh):
    return jax.shard_map(
        per_device,
        mesh=mesh,
        in_specs=(
            P(("groups", "fsdp"), "segment"),
            P("groups"),
            P(),
            P("fsdp", "segment", None, None, None),
            P("fsdp", "segment", None, None),
            P(),
            P(),
            P(),
        ),
        out_specs=(
            P(("groups", "fsdp"), "segment"),
            P(("groups", "fsdp"), "segment", None, None, None),
            P(("groups", "fsdp"), "segment", None, None),
        ),
        check_vma=False,
    )
```

```python
import jax
import jax.numpy as jnp
from jax import lax
from jax.sharding import PartitionSpec as P

PIPE = 2
HI = lax.Precision.HIGHEST
HOT = lax.Precision.HIGH


def bits_of(size):
    return size.bit_length() - 1


def swapped(x, axis, bit):
    size = lax.axis_size(axis)
    return lax.ppermute(x, axis, [(i, i ^ (1 << bit)) for i in range(size)])


def all_sum(x, axis, levels):
    for bit in range(levels):
        x = x + swapped(x, axis, bit)
    return x


def gather_along(x, axis, index, levels, dim):
    for bit in range(levels):
        other = swapped(x, axis, bit)
        upper = (index >> bit) & 1 == 1
        x = jnp.where(
            upper,
            jnp.concatenate([other, x], axis=dim),
            jnp.concatenate([x, other], axis=dim),
        )
    return x


def scatter_along(x, axis, index, levels, dim):
    for bit in reversed(range(levels)):
        half = x.shape[dim] // 2
        upper = (index >> bit) & 1
        keep = lax.dynamic_slice_in_dim(x, upper * half, half, axis=dim)
        send = lax.dynamic_slice_in_dim(x, (1 - upper) * half, half, axis=dim)
        x = keep + swapped(send, axis, bit)
    return x


def scatter_blocks(x, axis, index, levels):
    x = x.reshape((2,) * levels + x.shape[1:])
    for bit in range(levels):
        pos = levels - 1 - bit
        mine = (index >> bit) & 1
        keep = lax.dynamic_index_in_dim(x, mine, pos, keepdims=False)
        send = lax.dynamic_index_in_dim(x, 1 - mine, pos, keepdims=False)
        x = keep + swapped(send, axis, bit)
    return x


def gather_blocks(x, axis, index, levels):
    for count, bit in enumerate(reversed(range(levels))):
        other = swapped(x, axis, bit)
        upper = (index >> bit) & 1 == 1
        x = jnp.where(
            upper, jnp.stack([other, x], axis=count), jnp.stack([x, other], axis=count)
        )
    return x.reshape((-1,) + x.shape[levels:])


DIRECT = 4


def shifted(x, axis, shift, group):
    size = lax.axis_size(axis)
    route = [(i, i - i % group + (i % group + shift) % group) for i in range(size)]
    return lax.ppermute(x, axis, route)


def scatter_any(x, axis, index, levels):
    n = 1 << levels
    if n > DIRECT:
        return scatter_blocks(x, axis, index, levels)
    total = lax.dynamic_index_in_dim(x, index, 0, keepdims=False)
    for shift in range(1, n):
        send = lax.dynamic_index_in_dim(x, (index + shift) % n, 0, keepdims=False)
        total = total + shifted(send, axis, shift, n)
    return total


def gather_any(x, axis, index, levels):
    n = 1 << levels
    if n > DIRECT:
        return gather_blocks(x, axis, index, levels)
    got = jnp.stack([x] + [shifted(x, axis, shift, n) for shift in range(1, n)])
    order = (index - jnp.arange(n, dtype=jnp.int32)) % n
    return jnp.take(got, order, axis=0)


def sum_any(x, axis, levels):
    n = 1 << levels
    if n > DIRECT:
        return all_sum(x, axis, levels)
    total = x
    for shift in range(1, n):
        total = total + shifted(x, axis, shift, n)
    return total


def per_device(
    layer_inputs, labels, head_weight, gate_up_store, down_store, kept_rows, owners, slots
):
    members = lax.axis_size("fsdp")
    places = lax.axis_size("segment")
    sections = places // PIPE
    member = lax.axis_index("fsdp")
    place = lax.axis_index("segment")
    segment = place // sections
    section = place % sections
    is_last = segment == PIPE - 1
    tok_rows, piece_width = layer_inputs.shape
    tokens = tok_rows * members
    width = piece_width * sections
    blk = gate_up_store.shape[-1]
    capacity = gate_up_store.shape[0]
    kept = kept_rows.shape[2]
    sec_cols = kept_rows.shape[1] // sections
    nrow = width // blk
    nblocks = sec_cols * kept

    first_col = section * sec_cols
    sec_rows = lax.dynamic_slice(kept_rows, (segment, first_col, 0), (1, sec_cols, kept))
    sec_owner = lax.dynamic_slice(owners, (segment, first_col, 0), (1, sec_cols, kept))
    sec_slot = lax.dynamic_slice(slots, (segment, first_col, 0), (1, sec_cols, kept))
    sec_rows = sec_rows.reshape(nblocks)
    mine = sec_owner.reshape(nblocks) == member
    block_col = jnp.arange(nblocks, dtype=jnp.int32) // kept
    hits = mine[None, :] & (
        sec_slot.reshape(nblocks)[None, :] == jnp.arange(capacity, dtype=jnp.int32)[:, None]
    )
    valid = jnp.any(hits, axis=1)
    slot_col = jnp.sum(jnp.where(hits, block_col[None, :], 0), axis=1)
    slot_row = jnp.sum(jnp.where(hits, sec_rows[None, :], 0), axis=1)
    col_hot = valid[:, None] & (slot_col[:, None] == jnp.arange(sec_cols, dtype=jnp.int32)[None, :])
    row_hot = valid[:, None] & (slot_row[:, None] == jnp.arange(nrow, dtype=jnp.int32)[None, :])
    col_f = col_hot.astype(jnp.float32)
    col_b = col_hot.astype(jnp.bfloat16)
    row_f = row_hot.astype(jnp.float32)
    row_b = row_hot.astype(jnp.bfloat16)

    w_pair = gate_up_store[:, 0]
    w_down = down_store[:, 0]

    fsdp_bits = bits_of(members)
    sec_bits = bits_of(sections)

    x_mine = gather_along(layer_inputs, "segment", section, sec_bits, 1)
    x_mine = gather_any(x_mine, "fsdp", member, fsdp_bits).reshape(tokens, width)
    x_sel = jnp.einsum("cr,trb->ctb", row_b, x_mine.reshape(tokens, nrow, blk))
    x_sel = x_sel.astype(jnp.bfloat16)

    gu_slot = jnp.einsum("cta,cgab->ctgb", x_sel, w_pair, preferred_element_type=jnp.float32)
    gu_part = jnp.einsum("cj,ctgb->gtjb", col_f, gu_slot, precision=HOT)
    head_rows = head_weight.reshape(nrow, blk)
    head_sel = jnp.einsum("cr,rd->cd", row_f, head_rows, precision=HI)
    head_hi = head_sel.astype(jnp.bfloat16)
    head_lo = (head_sel - head_hi.astype(jnp.float32)).astype(jnp.bfloat16)
    head_two = jnp.stack([head_hi, head_lo], axis=1)
    folded = jnp.einsum(
        "chd,ckd->chk", w_down, head_two, preferred_element_type=jnp.float32
    ).sum(axis=2)
    f_part = jnp.einsum("cj,ch->jh", col_f, folded, precision=HOT)
    cols_per = sec_cols // members
    packed = gu_part.reshape(2 * tokens, members, cols_per, blk).transpose(1, 0, 2, 3)
    packed = scatter_any(packed, "fsdp", member, fsdp_bits)
    gate = packed[:tokens]
    up = packed[tokens:]
    f_sum = scatter_any(f_part.reshape(members, cols_per, blk), "fsdp", member, fsdp_bits)
    sig = jax.nn.sigmoid(gate)
    hidden_own = (gate * sig * up).astype(jnp.bfloat16)

    branch = jnp.einsum("tjh,jh->t", hidden_own.astype(jnp.float32), f_sum, precision=HI)
    x_term = jnp.einsum("td,d->t", x_mine.astype(jnp.float32), head_weight, precision=HI)
    branch = branch + jnp.where((section == 0) & (member == 0), x_term, 0.0)
    logits = sum_any(branch, "fsdp", fsdp_bits)
    logits = sum_any(logits, "segment", sec_bits) * width ** (-0.5)
    dlogit = jax.nn.sigmoid(logits) - labels.astype(jnp.float32)
    dout_last = (dlogit[:, None] * head_weight[None, :]).astype(jnp.bfloat16)

    def gate_grads(dhidden):
        dgate = (dhidden * up * sig * (1.0 + gate * (1.0 - sig))).astype(jnp.bfloat16)
        dup = (dhidden * gate * sig).astype(jnp.bfloat16)
        return dgate, dup

    def share(parts):
        whole = gather_any(jnp.stack(parts), "fsdp", member, fsdp_bits)
        n = len(parts)
        return whole.transpose(1, 2, 0, 3, 4).reshape(n, tokens, sec_cols, blk)

    def select_pair(dgate, dup):
        pair = jnp.stack([dgate, dup], axis=2)
        return jnp.einsum("cj,tjgb->ctgb", col_b, pair).astype(jnp.bfloat16)

    def spread_rows(d_sel):
        spread = jnp.einsum(
            "ctgb,cgab->cta", d_sel, w_pair, preferred_element_type=jnp.float32
        )
        return jnp.einsum("cr,cta->tra", row_f, spread, precision=HOT).reshape(tokens, width)

    dgate_last, dup_last = gate_grads(dlogit[:, None, None] * f_sum[None])
    shared = share([hidden_own, dgate_last, dup_last])
    hidden = shared[0]
    d_sel_last = select_pair(shared[1], shared[2])
    part_last = spread_rows(d_sel_last).reshape(members, tok_rows, width)
    rows_last = scatter_any(part_last, "fsdp", member, fsdp_bits)
    rows_last = sum_any(rows_last, "segment", sec_bits)
    rows_at = member * tok_rows
    cols_at = section * piece_width
    dout_rows = lax.dynamic_slice_in_dim(dout_last, rows_at, tok_rows, axis=0)
    grad_last = (dout_rows.astype(jnp.float32) + rows_last).astype(jnp.bfloat16)
    handed = lax.ppermute(
        grad_last, "segment", [(i, i - sections) for i in range(sections, places)]
    )
    first_rows = jnp.where(is_last, grad_last, handed)
    dout_first = gather_any(first_rows, "fsdp", member, fsdp_bits).reshape(tokens, width)

    dout_sel = jnp.einsum("cr,trd->ctd", row_b, dout_first.reshape(tokens, nrow, blk))
    dout_sel = dout_sel.astype(jnp.bfloat16)
    dh_slot = jnp.einsum("ctd,chd->cth", dout_sel, w_down, preferred_element_type=jnp.float32)
    dh_part = jnp.einsum("cj,cth->tjh", col_f, dh_slot, precision=HOT)
    dh_part = dh_part.reshape(tokens, members, cols_per, blk).transpose(1, 0, 2, 3)
    dhidden_first = scatter_any(dh_part, "fsdp", member, fsdp_bits)
    dgate_first, dup_first = gate_grads(dhidden_first)
    shared_first = share([dgate_first, dup_first])
    cot_sel = jnp.where(
        is_last,
        jnp.einsum("cr,trd->ctd", row_b, dout_last.reshape(tokens, nrow, blk)).astype(
            jnp.bfloat16
        ),
        dout_sel,
    )
    hid_sel = jnp.einsum("cj,tjh->cth", col_b, hidden).astype(jnp.bfloat16)
    grad_down = jnp.einsum(
        "cth,ctd->chd", hid_sel, cot_sel, preferred_element_type=jnp.float32
    ).astype(jnp.bfloat16)
    zero_bf = jnp.zeros((), jnp.bfloat16)
    grad_down = jnp.where(valid[:, None, None], grad_down, zero_bf)
    grad_down, shared_first = lax.optimization_barrier((grad_down, shared_first))
    d_sel_first = select_pair(shared_first[0], shared_first[1])
    part_first = spread_rows(d_sel_first).reshape(members, tok_rows, width)
    part_first = scatter_any(part_first, "fsdp", member, fsdp_bits)
    part_first = part_first.reshape(tok_rows, sections, piece_width).transpose(1, 0, 2)
    part_first = scatter_any(part_first, "segment", section, sec_bits)

    own_last = lax.dynamic_slice_in_dim(grad_last, cols_at, piece_width, axis=1)
    own_dout = lax.dynamic_slice(dout_first, (rows_at, cols_at), (tok_rows, piece_width))
    grad_first = (own_dout.astype(jnp.float32) + part_first).astype(jnp.bfloat16)
    input_grads = jnp.where(is_last, own_last, grad_first)

    d_sel = jnp.where(is_last, d_sel_last, d_sel_first)
    x_pair = jnp.broadcast_to(x_sel[:, None], (capacity, 2, tokens, blk))
    grad_pair = jnp.einsum(
        "cgta,cgtb->cgab", x_pair, d_sel.transpose(0, 2, 1, 3),
        preferred_element_type=jnp.float32,
    ).astype(jnp.bfloat16)
    grad_pair = jnp.where(valid[:, None, None, None], grad_pair, zero_bf)
    return (input_grads, grad_pair[:, None], grad_down[:, None])


def solution(mesh):
    return jax.shard_map(
        per_device,
        mesh=mesh,
        in_specs=(
            P(("groups", "fsdp"), "segment"),
            P("groups"),
            P(),
            P("fsdp", "segment", None, None, None),
            P("fsdp", "segment", None, None),
            P(),
            P(),
            P(),
        ),
        out_specs=(
            P(("groups", "fsdp"), "segment"),
            P(("groups", "fsdp"), "segment", None, None, None),
            P(("groups", "fsdp"), "segment", None, None),
        ),
        check_vma=False,
    )
```

```python
import jax
import jax.numpy as jnp
from jax import lax
from jax.sharding import PartitionSpec as P

PIPE = 2
HI = lax.Precision.HIGHEST
HOT = lax.Precision.HIGH


def bits_of(size):
    return size.bit_length() - 1


def swapped(x, axis, bit):
    size = lax.axis_size(axis)
    return lax.ppermute(x, axis, [(i, i ^ (1 << bit)) for i in range(size)])


def all_sum(x, axis, levels):
    for bit in range(levels):
        x = x + swapped(x, axis, bit)
    return x


def gather_along(x, axis, index, levels, dim):
    for bit in range(levels):
        other = swapped(x, axis, bit)
        upper = (index >> bit) & 1 == 1
        x = jnp.where(
            upper,
            jnp.concatenate([other, x], axis=dim),
            jnp.concatenate([x, other], axis=dim),
        )
    return x


def scatter_along(x, axis, index, levels, dim):
    for bit in reversed(range(levels)):
        half = x.shape[dim] // 2
        upper = (index >> bit) & 1
        keep = lax.dynamic_slice_in_dim(x, upper * half, half, axis=dim)
        send = lax.dynamic_slice_in_dim(x, (1 - upper) * half, half, axis=dim)
        x = keep + swapped(send, axis, bit)
    return x


def scatter_blocks(x, axis, index, levels):
    x = x.reshape((2,) * levels + x.shape[1:])
    for bit in range(levels):
        pos = levels - 1 - bit
        mine = (index >> bit) & 1
        keep = lax.dynamic_index_in_dim(x, mine, pos, keepdims=False)
        send = lax.dynamic_index_in_dim(x, 1 - mine, pos, keepdims=False)
        x = keep + swapped(send, axis, bit)
    return x


def gather_blocks(x, axis, index, levels):
    for count, bit in enumerate(reversed(range(levels))):
        other = swapped(x, axis, bit)
        upper = (index >> bit) & 1 == 1
        x = jnp.where(
            upper, jnp.stack([other, x], axis=count), jnp.stack([x, other], axis=count)
        )
    return x.reshape((-1,) + x.shape[levels:])


DIRECT = 4


def shifted(x, axis, shift, group):
    size = lax.axis_size(axis)
    route = [(i, i - i % group + (i % group + shift) % group) for i in range(size)]
    return lax.ppermute(x, axis, route)


def scatter_any(x, axis, index, levels):
    n = 1 << levels
    if n > DIRECT:
        return scatter_blocks(x, axis, index, levels)
    total = lax.dynamic_index_in_dim(x, index, 0, keepdims=False)
    for shift in range(1, n):
        send = lax.dynamic_index_in_dim(x, (index + shift) % n, 0, keepdims=False)
        total = total + shifted(send, axis, shift, n)
    return total


def gather_any(x, axis, index, levels):
    n = 1 << levels
    if n > DIRECT:
        return gather_blocks(x, axis, index, levels)
    got = jnp.stack([x] + [shifted(x, axis, shift, n) for shift in range(1, n)])
    order = (index - jnp.arange(n, dtype=jnp.int32)) % n
    return jnp.take(got, order, axis=0)


def sum_any(x, axis, levels):
    n = 1 << levels
    if n > DIRECT:
        return all_sum(x, axis, levels)
    total = x
    for shift in range(1, n):
        total = total + shifted(x, axis, shift, n)
    return total


def per_device(
    layer_inputs, labels, head_weight, gate_up_store, down_store, kept_rows, owners, slots
):
    members = lax.axis_size("fsdp")
    places = lax.axis_size("segment")
    sections = places // PIPE
    member = lax.axis_index("fsdp")
    place = lax.axis_index("segment")
    segment = place // sections
    section = place % sections
    is_last = segment == PIPE - 1
    tok_rows, piece_width = layer_inputs.shape
    tokens = tok_rows * members
    width = piece_width * sections
    blk = gate_up_store.shape[-1]
    capacity = gate_up_store.shape[0]
    kept = kept_rows.shape[2]
    sec_cols = kept_rows.shape[1] // sections
    nrow = width // blk
    nblocks = sec_cols * kept

    first_col = section * sec_cols
    sec_rows = lax.dynamic_slice(kept_rows, (segment, first_col, 0), (1, sec_cols, kept))
    sec_owner = lax.dynamic_slice(owners, (segment, first_col, 0), (1, sec_cols, kept))
    sec_slot = lax.dynamic_slice(slots, (segment, first_col, 0), (1, sec_cols, kept))
    sec_rows = sec_rows.reshape(nblocks)
    mine = sec_owner.reshape(nblocks) == member
    block_col = jnp.arange(nblocks, dtype=jnp.int32) // kept
    hits = mine[None, :] & (
        sec_slot.reshape(nblocks)[None, :] == jnp.arange(capacity, dtype=jnp.int32)[:, None]
    )
    valid = jnp.any(hits, axis=1)
    slot_col = jnp.sum(jnp.where(hits, block_col[None, :], 0), axis=1)
    slot_row = jnp.sum(jnp.where(hits, sec_rows[None, :], 0), axis=1)
    col_hot = valid[:, None] & (slot_col[:, None] == jnp.arange(sec_cols, dtype=jnp.int32)[None, :])
    row_hot = valid[:, None] & (slot_row[:, None] == jnp.arange(nrow, dtype=jnp.int32)[None, :])
    col_f = col_hot.astype(jnp.float32)
    col_b = col_hot.astype(jnp.bfloat16)
    row_f = row_hot.astype(jnp.float32)
    row_b = row_hot.astype(jnp.bfloat16)

    w_pair = gate_up_store[:, 0]
    w_down = down_store[:, 0]

    fsdp_bits = bits_of(members)
    sec_bits = bits_of(sections)

    x_mine = gather_along(layer_inputs, "segment", section, sec_bits, 1)
    x_mine = gather_any(x_mine, "fsdp", member, fsdp_bits).reshape(tokens, width)
    x_sel = jnp.einsum("cr,trb->ctb", row_b, x_mine.reshape(tokens, nrow, blk))
    x_sel = x_sel.astype(jnp.bfloat16)

    gu_slot = jnp.einsum("cta,cgab->ctgb", x_sel, w_pair, preferred_element_type=jnp.float32)
    gu_part = jnp.einsum("cj,ctgb->gtjb", col_f, gu_slot, precision=HOT)
    head_rows = head_weight.reshape(nrow, blk)
    head_sel = jnp.einsum("cr,rd->cd", row_f, head_rows, precision=HI)
    gu_part, head_sel = lax.optimization_barrier((gu_part, head_sel))
    head_hi = head_sel.astype(jnp.bfloat16)
    head_lo = (head_sel - head_hi.astype(jnp.float32)).astype(jnp.bfloat16)
    head_two = jnp.stack([head_hi, head_lo], axis=1)
    folded = jnp.einsum(
        "chd,ckd->chk", w_down, head_two, preferred_element_type=jnp.float32
    ).sum(axis=2)
    f_part = jnp.einsum("cj,ch->jh", col_f, folded, precision=HOT)
    cols_per = sec_cols // members
    packed = gu_part.reshape(2 * tokens, members, cols_per, blk).transpose(1, 0, 2, 3)
    packed = scatter_any(packed, "fsdp", member, fsdp_bits)
    gate = packed[:tokens]
    up = packed[tokens:]
    f_sum = scatter_any(f_part.reshape(members, cols_per, blk), "fsdp", member, fsdp_bits)
    sig = jax.nn.sigmoid(gate)
    hidden_own = (gate * sig * up).astype(jnp.bfloat16)

    branch = jnp.einsum("tjh,jh->t", hidden_own.astype(jnp.float32), f_sum, precision=HI)
    x_term = jnp.einsum("td,d->t", x_mine.astype(jnp.float32), head_weight, precision=HI)
    branch = branch + jnp.where((section == 0) & (member == 0), x_term, 0.0)
    logits = sum_any(branch, "fsdp", fsdp_bits)
    logits = sum_any(logits, "segment", sec_bits) * width ** (-0.5)
    dlogit = jax.nn.sigmoid(logits) - labels.astype(jnp.float32)
    dout_last = (dlogit[:, None] * head_weight[None, :]).astype(jnp.bfloat16)

    def gate_grads(dhidden):
        dgate = (dhidden * up * sig * (1.0 + gate * (1.0 - sig))).astype(jnp.bfloat16)
        dup = (dhidden * gate * sig).astype(jnp.bfloat16)
        return dgate, dup

    def share(parts):
        whole = gather_any(jnp.stack(parts), "fsdp", member, fsdp_bits)
        n = len(parts)
        return whole.transpose(1, 2, 0, 3, 4).reshape(n, tokens, sec_cols, blk)

    def select_pair(dgate, dup):
        pair = jnp.stack([dgate, dup], axis=2)
        return jnp.einsum("cj,tjgb->ctgb", col_b, pair).astype(jnp.bfloat16)

    def spread_rows(d_sel):
        spread = jnp.einsum(
            "ctgb,cgab->cta", d_sel, w_pair, preferred_element_type=jnp.float32
        )
        return jnp.einsum("cr,cta->tra", row_f, spread, precision=HOT).reshape(tokens, width)

    dgate_last, dup_last = gate_grads(dlogit[:, None, None] * f_sum[None])
    shared = share([hidden_own, dgate_last, dup_last])
    hidden = shared[0]
    d_sel_last = select_pair(shared[1], shared[2])
    part_last = spread_rows(d_sel_last).reshape(members, tok_rows, width)
    rows_last = scatter_any(part_last, "fsdp", member, fsdp_bits)
    rows_last = sum_any(rows_last, "segment", sec_bits)
    rows_at = member * tok_rows
    cols_at = section * piece_width
    dout_rows = lax.dynamic_slice_in_dim(dout_last, rows_at, tok_rows, axis=0)
    grad_last = (dout_rows.astype(jnp.float32) + rows_last).astype(jnp.bfloat16)
    handed = lax.ppermute(
        grad_last, "segment", [(i, i - sections) for i in range(sections, places)]
    )
    first_rows = jnp.where(is_last, grad_last, handed)
    dout_first = gather_any(first_rows, "fsdp", member, fsdp_bits).reshape(tokens, width)

    dout_sel = jnp.einsum("cr,trd->ctd", row_b, dout_first.reshape(tokens, nrow, blk))
    dout_sel = dout_sel.astype(jnp.bfloat16)
    dh_slot = jnp.einsum("ctd,chd->cth", dout_sel, w_down, preferred_element_type=jnp.float32)
    dh_part = jnp.einsum("cj,cth->tjh", col_f, dh_slot, precision=HOT)
    dh_part = dh_part.reshape(tokens, members, cols_per, blk).transpose(1, 0, 2, 3)
    cot_sel = jnp.where(
        is_last,
        jnp.einsum("cr,trd->ctd", row_b, dout_last.reshape(tokens, nrow, blk)).astype(
            jnp.bfloat16
        ),
        dout_sel,
    )
    hid_sel = jnp.einsum("cj,tjh->cth", col_b, hidden).astype(jnp.bfloat16)
    dh_part, hid_sel, cot_sel = lax.optimization_barrier((dh_part, hid_sel, cot_sel))
    dhidden_first = scatter_any(dh_part, "fsdp", member, fsdp_bits)
    grad_down = jnp.einsum(
        "cth,ctd->chd", hid_sel, cot_sel, preferred_element_type=jnp.float32
    ).astype(jnp.bfloat16)
    zero_bf = jnp.zeros((), jnp.bfloat16)
    grad_down = jnp.where(valid[:, None, None], grad_down, zero_bf)
    dgate_first, dup_first = gate_grads(dhidden_first)
    shared_first = share([dgate_first, dup_first])
    grad_down, shared_first = lax.optimization_barrier((grad_down, shared_first))
    d_sel_first = select_pair(shared_first[0], shared_first[1])
    part_first = spread_rows(d_sel_first).reshape(members, tok_rows, width)
    part_first = scatter_any(part_first, "fsdp", member, fsdp_bits)
    part_first = part_first.reshape(tok_rows, sections, piece_width).transpose(1, 0, 2)
    part_first = scatter_any(part_first, "segment", section, sec_bits)

    own_last = lax.dynamic_slice_in_dim(grad_last, cols_at, piece_width, axis=1)
    own_dout = lax.dynamic_slice(dout_first, (rows_at, cols_at), (tok_rows, piece_width))
    grad_first = (own_dout.astype(jnp.float32) + part_first).astype(jnp.bfloat16)
    input_grads = jnp.where(is_last, own_last, grad_first)

    d_sel = jnp.where(is_last, d_sel_last, d_sel_first)
    x_pair = jnp.broadcast_to(x_sel[:, None], (capacity, 2, tokens, blk))
    grad_pair = jnp.einsum(
        "cgta,cgtb->cgab", x_pair, d_sel.transpose(0, 2, 1, 3),
        preferred_element_type=jnp.float32,
    ).astype(jnp.bfloat16)
    grad_pair = jnp.where(valid[:, None, None, None], grad_pair, zero_bf)
    return (input_grads, grad_pair[:, None], grad_down[:, None])


def solution(mesh):
    return jax.shard_map(
        per_device,
        mesh=mesh,
        in_specs=(
            P(("groups", "fsdp"), "segment"),
            P("groups"),
            P(),
            P("fsdp", "segment", None, None, None),
            P("fsdp", "segment", None, None),
            P(),
            P(),
            P(),
        ),
        out_specs=(
            P(("groups", "fsdp"), "segment"),
            P(("groups", "fsdp"), "segment", None, None, None),
            P(("groups", "fsdp"), "segment", None, None),
        ),
        check_vma=False,
    )
```

```python
import jax
import jax.numpy as jnp
from jax import lax
from jax.experimental import pallas as pl
from jax.sharding import PartitionSpec as P

PIPE = 2
HI = lax.Precision.HIGHEST
HOT = lax.Precision.HIGH


def bits_of(size):
    return size.bit_length() - 1


def swapped(x, axis, bit):
    size = lax.axis_size(axis)
    return lax.ppermute(x, axis, [(i, i ^ (1 << bit)) for i in range(size)])


def all_sum(x, axis, levels):
    for bit in range(levels):
        x = x + swapped(x, axis, bit)
    return x


def gather_along(x, axis, index, levels, dim):
    for bit in range(levels):
        other = swapped(x, axis, bit)
        upper = (index >> bit) & 1 == 1
        x = jnp.where(
            upper,
            jnp.concatenate([other, x], axis=dim),
            jnp.concatenate([x, other], axis=dim),
        )
    return x


def scatter_along(x, axis, index, levels, dim):
    for bit in reversed(range(levels)):
        half = x.shape[dim] // 2
        upper = (index >> bit) & 1
        keep = lax.dynamic_slice_in_dim(x, upper * half, half, axis=dim)
        send = lax.dynamic_slice_in_dim(x, (1 - upper) * half, half, axis=dim)
        x = keep + swapped(send, axis, bit)
    return x


def scatter_blocks(x, axis, index, levels):
    x = x.reshape((2,) * levels + x.shape[1:])
    for bit in range(levels):
        pos = levels - 1 - bit
        mine = (index >> bit) & 1
        keep = lax.dynamic_index_in_dim(x, mine, pos, keepdims=False)
        send = lax.dynamic_index_in_dim(x, 1 - mine, pos, keepdims=False)
        x = keep + swapped(send, axis, bit)
    return x


def gather_blocks(x, axis, index, levels):
    for count, bit in enumerate(reversed(range(levels))):
        other = swapped(x, axis, bit)
        upper = (index >> bit) & 1 == 1
        x = jnp.where(
            upper, jnp.stack([other, x], axis=count), jnp.stack([x, other], axis=count)
        )
    return x.reshape((-1,) + x.shape[levels:])


DIRECT = 4


def shifted(x, axis, shift, group):
    size = lax.axis_size(axis)
    route = [(i, i - i % group + (i % group + shift) % group) for i in range(size)]
    return lax.ppermute(x, axis, route)


def scatter_any(x, axis, index, levels):
    n = 1 << levels
    if n > DIRECT:
        return scatter_blocks(x, axis, index, levels)
    total = lax.dynamic_index_in_dim(x, index, 0, keepdims=False)
    for shift in range(1, n):
        send = lax.dynamic_index_in_dim(x, (index + shift) % n, 0, keepdims=False)
        total = total + shifted(send, axis, shift, n)
    return total


def gather_any(x, axis, index, levels):
    n = 1 << levels
    if n > DIRECT:
        return gather_blocks(x, axis, index, levels)
    got = jnp.stack([x] + [shifted(x, axis, shift, n) for shift in range(1, n)])
    order = (index - jnp.arange(n, dtype=jnp.int32)) % n
    return jnp.take(got, order, axis=0)


def sum_any(x, axis, levels):
    n = 1 << levels
    if n > DIRECT:
        return all_sum(x, axis, levels)
    total = x
    for shift in range(1, n):
        total = total + shifted(x, axis, shift, n)
    return total


def slot_step(capacity):
    for step in range(16, 0, -1):
        if capacity % step == 0:
            return step
    return 1


def spec(shape):
    rank = len(shape)
    return pl.BlockSpec(shape, lambda i: (i,) + (0,) * (rank - 1))


def slot_nn(x, w):
    cap, tok, k = x.shape
    groups, n = w.shape[1], w.shape[3]
    step = slot_step(cap)

    def body(x_ref, w_ref, o_ref):
        for s in range(step):
            for g in range(groups):
                o_ref[s, g] = jnp.dot(x_ref[s], w_ref[s, g], preferred_element_type=jnp.float32)

    return pl.pallas_call(
        body,
        grid=(cap // step,),
        in_specs=[spec((step, tok, k)), spec((step, groups, k, n))],
        out_specs=spec((step, groups, tok, n)),
        out_shape=jax.ShapeDtypeStruct((cap, groups, tok, n), jnp.float32),
    )(x, w)


def slot_nt(d, w):
    cap, groups, tok, n = d.shape
    k = w.shape[2]
    step = slot_step(cap)
    dims = (((1,), (1,)), ((), ()))

    def body(d_ref, w_ref, o_ref):
        for s in range(step):
            acc = lax.dot_general(d_ref[s, 0], w_ref[s, 0], dims, preferred_element_type=jnp.float32)
            for g in range(1, groups):
                acc = acc + lax.dot_general(
                    d_ref[s, g], w_ref[s, g], dims, preferred_element_type=jnp.float32
                )
            o_ref[s] = acc

    return pl.pallas_call(
        body,
        grid=(cap // step,),
        in_specs=[spec((step, groups, tok, n)), spec((step, groups, k, n))],
        out_specs=spec((step, tok, k)),
        out_shape=jax.ShapeDtypeStruct((cap, tok, k), jnp.float32),
    )(d, w)


def slot_tn(xt, d):
    cap, k, tok = xt.shape
    groups, n = d.shape[1], d.shape[3]
    step = slot_step(cap)

    def body(x_ref, d_ref, o_ref):
        for s in range(step):
            for g in range(groups):
                o_ref[s, g] = jnp.dot(
                    x_ref[s], d_ref[s, g], preferred_element_type=jnp.float32
                ).astype(o_ref.dtype)

    return pl.pallas_call(
        body,
        grid=(cap // step,),
        in_specs=[spec((step, k, tok)), spec((step, groups, tok, n))],
        out_specs=spec((step, groups, k, n)),
        out_shape=jax.ShapeDtypeStruct((cap, groups, k, n), jnp.bfloat16),
    )(xt, d)


def per_device(
    layer_inputs, labels, head_weight, gate_up_store, down_store, kept_rows, owners, slots
):
    members = lax.axis_size("fsdp")
    places = lax.axis_size("segment")
    sections = places // PIPE
    member = lax.axis_index("fsdp")
    place = lax.axis_index("segment")
    segment = place // sections
    section = place % sections
    is_last = segment == PIPE - 1
    tok_rows, piece_width = layer_inputs.shape
    tokens = tok_rows * members
    width = piece_width * sections
    blk = gate_up_store.shape[-1]
    capacity = gate_up_store.shape[0]
    kept = kept_rows.shape[2]
    sec_cols = kept_rows.shape[1] // sections
    nrow = width // blk
    nblocks = sec_cols * kept

    first_col = section * sec_cols
    sec_rows = lax.dynamic_slice(kept_rows, (segment, first_col, 0), (1, sec_cols, kept))
    sec_owner = lax.dynamic_slice(owners, (segment, first_col, 0), (1, sec_cols, kept))
    sec_slot = lax.dynamic_slice(slots, (segment, first_col, 0), (1, sec_cols, kept))
    sec_rows = sec_rows.reshape(nblocks)
    mine = sec_owner.reshape(nblocks) == member
    block_col = jnp.arange(nblocks, dtype=jnp.int32) // kept
    hits = mine[None, :] & (
        sec_slot.reshape(nblocks)[None, :] == jnp.arange(capacity, dtype=jnp.int32)[:, None]
    )
    valid = jnp.any(hits, axis=1)
    slot_col = jnp.sum(jnp.where(hits, block_col[None, :], 0), axis=1)
    slot_row = jnp.sum(jnp.where(hits, sec_rows[None, :], 0), axis=1)
    col_hot = valid[:, None] & (slot_col[:, None] == jnp.arange(sec_cols, dtype=jnp.int32)[None, :])
    row_hot = valid[:, None] & (slot_row[:, None] == jnp.arange(nrow, dtype=jnp.int32)[None, :])
    col_f = col_hot.astype(jnp.float32)
    col_b = col_hot.astype(jnp.bfloat16)
    row_f = row_hot.astype(jnp.float32)
    row_b = row_hot.astype(jnp.bfloat16)

    w_pair = gate_up_store[:, 0]
    w_down = down_store[:, 0]

    fsdp_bits = bits_of(members)
    sec_bits = bits_of(sections)

    x_mine = gather_along(layer_inputs, "segment", section, sec_bits, 1)
    x_mine = gather_any(x_mine, "fsdp", member, fsdp_bits).reshape(tokens, width)
    x_sel = jnp.einsum("cr,trb->ctb", row_b, x_mine.reshape(tokens, nrow, blk))
    x_sel = x_sel.astype(jnp.bfloat16)

    gu_slot = slot_nn(x_sel, w_pair)
    gu_part = jnp.einsum("cj,cgtb->gtjb", col_f, gu_slot, precision=HOT)
    head_rows = head_weight.reshape(nrow, blk)
    head_sel = jnp.einsum("cr,rd->cd", row_f, head_rows, precision=HI)
    gu_part, head_sel = lax.optimization_barrier((gu_part, head_sel))
    head_hi = head_sel.astype(jnp.bfloat16)
    head_lo = (head_sel - head_hi.astype(jnp.float32)).astype(jnp.bfloat16)
    head_two = jnp.stack([head_hi, head_lo], axis=1)
    folded = jnp.einsum(
        "chd,ckd->chk", w_down, head_two, preferred_element_type=jnp.float32
    ).sum(axis=2)
    f_part = jnp.einsum("cj,ch->jh", col_f, folded, precision=HOT)
    cols_per = sec_cols // members
    packed = gu_part.reshape(2 * tokens, members, cols_per, blk).transpose(1, 0, 2, 3)
    packed = scatter_any(packed, "fsdp", member, fsdp_bits)
    gate = packed[:tokens]
    up = packed[tokens:]
    f_sum = scatter_any(f_part.reshape(members, cols_per, blk), "fsdp", member, fsdp_bits)
    sig = jax.nn.sigmoid(gate)
    hidden_own = (gate * sig * up).astype(jnp.bfloat16)

    branch = jnp.einsum("tjh,jh->t", hidden_own.astype(jnp.float32), f_sum, precision=HI)
    x_term = jnp.einsum("td,d->t", x_mine.astype(jnp.float32), head_weight, precision=HI)
    branch = branch + jnp.where((section == 0) & (member == 0), x_term, 0.0)
    logits = sum_any(branch, "fsdp", fsdp_bits)
    logits = sum_any(logits, "segment", sec_bits) * width ** (-0.5)
    dlogit = jax.nn.sigmoid(logits) - labels.astype(jnp.float32)
    dout_last = (dlogit[:, None] * head_weight[None, :]).astype(jnp.bfloat16)

    def gate_grads(dhidden):
        dgate = (dhidden * up * sig * (1.0 + gate * (1.0 - sig))).astype(jnp.bfloat16)
        dup = (dhidden * gate * sig).astype(jnp.bfloat16)
        return dgate, dup

    def share(parts):
        whole = gather_any(jnp.stack(parts), "fsdp", member, fsdp_bits)
        n = len(parts)
        return whole.transpose(1, 2, 0, 3, 4).reshape(n, tokens, sec_cols, blk)

    def select_pair(dgate, dup):
        pair = jnp.stack([dgate, dup], axis=2)
        return jnp.einsum("cj,tjgb->cgtb", col_b, pair).astype(jnp.bfloat16)

    def spread_rows(d_sel):
        spread = slot_nt(d_sel, w_pair)
        return jnp.einsum("cr,cta->tra", row_f, spread, precision=HOT).reshape(tokens, width)

    dgate_last, dup_last = gate_grads(dlogit[:, None, None] * f_sum[None])
    shared = share([hidden_own, dgate_last, dup_last])
    hidden = shared[0]
    d_sel_last = select_pair(shared[1], shared[2])
    part_last = spread_rows(d_sel_last).reshape(members, tok_rows, width)
    rows_last = scatter_any(part_last, "fsdp", member, fsdp_bits)
    rows_last = sum_any(rows_last, "segment", sec_bits)
    rows_at = member * tok_rows
    cols_at = section * piece_width
    dout_rows = lax.dynamic_slice_in_dim(dout_last, rows_at, tok_rows, axis=0)
    grad_last = (dout_rows.astype(jnp.float32) + rows_last).astype(jnp.bfloat16)
    handed = lax.ppermute(
        grad_last, "segment", [(i, i - sections) for i in range(sections, places)]
    )
    first_rows = jnp.where(is_last, grad_last, handed)
    dout_first = gather_any(first_rows, "fsdp", member, fsdp_bits).reshape(tokens, width)

    dout_sel = jnp.einsum("cr,trd->ctd", row_b, dout_first.reshape(tokens, nrow, blk))
    dout_sel = dout_sel.astype(jnp.bfloat16)
    dh_slot = slot_nt(dout_sel[:, None], w_down[:, None])
    dh_part = jnp.einsum("cj,cth->tjh", col_f, dh_slot, precision=HOT)
    dh_part = dh_part.reshape(tokens, members, cols_per, blk).transpose(1, 0, 2, 3)
    cot_sel = jnp.where(
        is_last,
        jnp.einsum("cr,trd->ctd", row_b, dout_last.reshape(tokens, nrow, blk)).astype(
            jnp.bfloat16
        ),
        dout_sel,
    )
    hid_sel = jnp.einsum("cj,tjh->cth", col_b, hidden).astype(jnp.bfloat16)
    dh_part, hid_sel, cot_sel = lax.optimization_barrier((dh_part, hid_sel, cot_sel))
    dhidden_first = scatter_any(dh_part, "fsdp", member, fsdp_bits)
    grad_down = slot_tn(hid_sel.transpose(0, 2, 1), cot_sel[:, None])[:, 0]
    dgate_first, dup_first = gate_grads(dhidden_first)
    shared_first = share([dgate_first, dup_first])
    grad_down, shared_first = lax.optimization_barrier((grad_down, shared_first))
    d_sel_first = select_pair(shared_first[0], shared_first[1])
    part_first = spread_rows(d_sel_first).reshape(members, tok_rows, width)
    part_first = scatter_any(part_first, "fsdp", member, fsdp_bits)
    part_first = part_first.reshape(tok_rows, sections, piece_width).transpose(1, 0, 2)
    part_first = scatter_any(part_first, "segment", section, sec_bits)

    own_last = lax.dynamic_slice_in_dim(grad_last, cols_at, piece_width, axis=1)
    own_dout = lax.dynamic_slice(dout_first, (rows_at, cols_at), (tok_rows, piece_width))
    grad_first = (own_dout.astype(jnp.float32) + part_first).astype(jnp.bfloat16)
    input_grads = jnp.where(is_last, own_last, grad_first)

    d_sel = jnp.where(is_last, d_sel_last, d_sel_first)
    grad_pair = slot_tn(x_sel.transpose(0, 2, 1), d_sel)
    return (input_grads, grad_pair[:, None], grad_down[:, None])


def solution(mesh):
    return jax.shard_map(
        per_device,
        mesh=mesh,
        in_specs=(
            P(("groups", "fsdp"), "segment"),
            P("groups"),
            P(),
            P("fsdp", "segment", None, None, None),
            P("fsdp", "segment", None, None),
            P(),
            P(),
            P(),
        ),
        out_specs=(
            P(("groups", "fsdp"), "segment"),
            P(("groups", "fsdp"), "segment", None, None, None),
            P(("groups", "fsdp"), "segment", None, None),
        ),
        check_vma=False,
    )
```

```python
import jax
import jax.numpy as jnp
from jax import lax
from jax.sharding import PartitionSpec as P

PIPE = 2
HI = lax.Precision.HIGHEST
HOT = lax.Precision.HIGH


def bits_of(size):
    return size.bit_length() - 1


def swapped(x, axis, bit):
    size = lax.axis_size(axis)
    return lax.ppermute(x, axis, [(i, i ^ (1 << bit)) for i in range(size)])


def all_sum(x, axis, levels):
    for bit in range(levels):
        x = x + swapped(x, axis, bit)
    return x


def gather_along(x, axis, index, levels, dim):
    for bit in range(levels):
        other = swapped(x, axis, bit)
        upper = (index >> bit) & 1 == 1
        x = jnp.where(
            upper,
            jnp.concatenate([other, x], axis=dim),
            jnp.concatenate([x, other], axis=dim),
        )
    return x


def scatter_along(x, axis, index, levels, dim):
    for bit in reversed(range(levels)):
        half = x.shape[dim] // 2
        upper = (index >> bit) & 1
        keep = lax.dynamic_slice_in_dim(x, upper * half, half, axis=dim)
        send = lax.dynamic_slice_in_dim(x, (1 - upper) * half, half, axis=dim)
        x = keep + swapped(send, axis, bit)
    return x


def scatter_blocks(x, axis, index, levels):
    x = x.reshape((2,) * levels + x.shape[1:])
    for bit in range(levels):
        pos = levels - 1 - bit
        mine = (index >> bit) & 1
        keep = lax.dynamic_index_in_dim(x, mine, pos, keepdims=False)
        send = lax.dynamic_index_in_dim(x, 1 - mine, pos, keepdims=False)
        x = keep + swapped(send, axis, bit)
    return x


def gather_blocks(x, axis, index, levels):
    for count, bit in enumerate(reversed(range(levels))):
        other = swapped(x, axis, bit)
        upper = (index >> bit) & 1 == 1
        x = jnp.where(
            upper, jnp.stack([other, x], axis=count), jnp.stack([x, other], axis=count)
        )
    return x.reshape((-1,) + x.shape[levels:])


DIRECT = 4


def shifted(x, axis, shift, group):
    size = lax.axis_size(axis)
    route = [(i, i - i % group + (i % group + shift) % group) for i in range(size)]
    return lax.ppermute(x, axis, route)


def scatter_any(x, axis, index, levels):
    n = 1 << levels
    if n > DIRECT:
        return scatter_blocks(x, axis, index, levels)
    total = lax.dynamic_index_in_dim(x, index, 0, keepdims=False)
    for shift in range(1, n):
        send = lax.dynamic_index_in_dim(x, (index + shift) % n, 0, keepdims=False)
        total = total + shifted(send, axis, shift, n)
    return total


def gather_any(x, axis, index, levels):
    n = 1 << levels
    if n > DIRECT:
        return gather_blocks(x, axis, index, levels)
    got = jnp.stack([x] + [shifted(x, axis, shift, n) for shift in range(1, n)])
    order = (index - jnp.arange(n, dtype=jnp.int32)) % n
    return jnp.take(got, order, axis=0)


def sum_any(x, axis, levels):
    n = 1 << levels
    if n > DIRECT:
        return all_sum(x, axis, levels)
    total = x
    for shift in range(1, n):
        total = total + shifted(x, axis, shift, n)
    return total


GRID = ("fsdp", "segment")


def grid_shift(x, members, places, sections, df, ds):
    route = []
    for f in range(members):
        for p in range(places):
            base, sec = p - p % sections, p % sections
            target = ((f + df) % members) * places + base + (sec + ds) % sections
            route.append((f * places + p, target))
    return lax.ppermute(x, GRID, route)


def grid_pairs(members, sections):
    return [(df, ds) for df in range(members) for ds in range(sections) if df or ds]


def gather_grid(x, members, places, sections, member, section):
    got = [[None] * sections for _ in range(members)]
    got[0][0] = x
    for df, ds in grid_pairs(members, sections):
        got[df][ds] = grid_shift(x, members, places, sections, df, ds)
    got = jnp.stack([jnp.stack(row) for row in got])
    by_f = (member - jnp.arange(members, dtype=jnp.int32)) % members
    by_s = (section - jnp.arange(sections, dtype=jnp.int32)) % sections
    return jnp.take(jnp.take(got, by_f, axis=0), by_s, axis=1)


def sum_grid(x, members, places, sections):
    total = x
    for df, ds in grid_pairs(members, sections):
        total = total + grid_shift(x, members, places, sections, df, ds)
    return total


def in_order(parts, index, count):
    got = jnp.stack(parts)
    got = jnp.take(got, (index - jnp.arange(count, dtype=jnp.int32)) % count, axis=0)
    total = got[0]
    for k in range(1, count):
        total = total + got[k]
    return total


def per_device(
    layer_inputs, labels, head_weight, gate_up_store, down_store, kept_rows, owners, slots
):
    members = lax.axis_size("fsdp")
    places = lax.axis_size("segment")
    sections = places // PIPE
    member = lax.axis_index("fsdp")
    place = lax.axis_index("segment")
    segment = place // sections
    section = place % sections
    is_last = segment == PIPE - 1
    tok_rows, piece_width = layer_inputs.shape
    tokens = tok_rows * members
    width = piece_width * sections
    blk = gate_up_store.shape[-1]
    capacity = gate_up_store.shape[0]
    kept = kept_rows.shape[2]
    sec_cols = kept_rows.shape[1] // sections
    nrow = width // blk
    nblocks = sec_cols * kept

    first_col = section * sec_cols
    sec_rows = lax.dynamic_slice(kept_rows, (segment, first_col, 0), (1, sec_cols, kept))
    sec_owner = lax.dynamic_slice(owners, (segment, first_col, 0), (1, sec_cols, kept))
    sec_slot = lax.dynamic_slice(slots, (segment, first_col, 0), (1, sec_cols, kept))
    sec_rows = sec_rows.reshape(nblocks)
    mine = sec_owner.reshape(nblocks) == member
    block_col = jnp.arange(nblocks, dtype=jnp.int32) // kept
    hits = mine[None, :] & (
        sec_slot.reshape(nblocks)[None, :] == jnp.arange(capacity, dtype=jnp.int32)[:, None]
    )
    valid = jnp.any(hits, axis=1)
    slot_col = jnp.sum(jnp.where(hits, block_col[None, :], 0), axis=1)
    slot_row = jnp.sum(jnp.where(hits, sec_rows[None, :], 0), axis=1)
    col_hot = valid[:, None] & (slot_col[:, None] == jnp.arange(sec_cols, dtype=jnp.int32)[None, :])
    row_hot = valid[:, None] & (slot_row[:, None] == jnp.arange(nrow, dtype=jnp.int32)[None, :])
    col_f = col_hot.astype(jnp.float32)
    col_b = col_hot.astype(jnp.bfloat16)
    row_f = row_hot.astype(jnp.float32)
    row_b = row_hot.astype(jnp.bfloat16)

    w_pair = gate_up_store[:, 0]
    w_down = down_store[:, 0]

    fsdp_bits = bits_of(members)
    sec_bits = bits_of(sections)

    small_grid = members * sections <= 2 * DIRECT
    if small_grid:
        x_mine = gather_grid(layer_inputs, members, places, sections, member, section)
        x_mine = x_mine.transpose(0, 2, 1, 3).reshape(tokens, width)
    else:
        x_mine = gather_along(layer_inputs, "segment", section, sec_bits, 1)
        x_mine = gather_any(x_mine, "fsdp", member, fsdp_bits).reshape(tokens, width)
    x_sel = jnp.einsum("cr,trb->ctb", row_b, x_mine.reshape(tokens, nrow, blk))
    x_sel = x_sel.astype(jnp.bfloat16)

    gu_slot = jnp.einsum("cta,cgab->ctgb", x_sel, w_pair, preferred_element_type=jnp.float32)
    gu_part = jnp.einsum("cj,ctgb->gtjb", col_f, gu_slot, precision=HOT)
    head_rows = head_weight.reshape(nrow, blk)
    head_sel = jnp.einsum("cr,rd->cd", row_f, head_rows, precision=HI)
    head_hi = head_sel.astype(jnp.bfloat16)
    head_lo = (head_sel - head_hi.astype(jnp.float32)).astype(jnp.bfloat16)
    head_two = jnp.stack([head_hi, head_lo], axis=1)
    folded = jnp.einsum(
        "chd,ckd->chk", w_down, head_two, preferred_element_type=jnp.float32
    ).sum(axis=2)
    f_part = jnp.einsum("cj,ch->jh", col_f, folded, precision=HOT)
    cols_per = sec_cols // members
    packed = gu_part.reshape(2 * tokens, members, cols_per, blk).transpose(1, 0, 2, 3)
    packed = scatter_any(packed, "fsdp", member, fsdp_bits)
    gate = packed[:tokens]
    up = packed[tokens:]
    f_sum = scatter_any(f_part.reshape(members, cols_per, blk), "fsdp", member, fsdp_bits)
    sig = jax.nn.sigmoid(gate)
    hidden_own = (gate * sig * up).astype(jnp.bfloat16)

    branch = jnp.einsum("tjh,jh->t", hidden_own.astype(jnp.float32), f_sum, precision=HI)
    x_term = jnp.einsum("td,d->t", x_mine.astype(jnp.float32), head_weight, precision=HI)
    branch = branch + jnp.where((section == 0) & (member == 0), x_term, 0.0)
    if small_grid:
        logits = sum_grid(branch, members, places, sections)
    else:
        logits = sum_any(sum_any(branch, "fsdp", fsdp_bits), "segment", sec_bits)
    logits = logits * width ** (-0.5)
    dlogit = jax.nn.sigmoid(logits) - labels.astype(jnp.float32)
    dout_last = (dlogit[:, None] * head_weight[None, :]).astype(jnp.bfloat16)

    def gate_grads(dhidden):
        dgate = (dhidden * up * sig * (1.0 + gate * (1.0 - sig))).astype(jnp.bfloat16)
        dup = (dhidden * gate * sig).astype(jnp.bfloat16)
        return dgate, dup

    def share(parts):
        whole = gather_any(jnp.stack(parts), "fsdp", member, fsdp_bits)
        n = len(parts)
        return whole.transpose(1, 2, 0, 3, 4).reshape(n, tokens, sec_cols, blk)

    def select_pair(dgate, dup):
        pair = jnp.stack([dgate, dup], axis=2)
        return jnp.einsum("cj,tjgb->ctgb", col_b, pair).astype(jnp.bfloat16)

    def spread_rows(d_sel):
        spread = jnp.einsum(
            "ctgb,cgab->cta", d_sel, w_pair, preferred_element_type=jnp.float32
        )
        return jnp.einsum("cr,cta->tra", row_f, spread, precision=HOT).reshape(tokens, width)

    dgate_last, dup_last = gate_grads(dlogit[:, None, None] * f_sum[None])
    shared = share([hidden_own, dgate_last, dup_last])
    hidden = shared[0]
    d_sel_last = select_pair(shared[1], shared[2])
    part_last = spread_rows(d_sel_last).reshape(members, tok_rows, width)
    rows_last = scatter_any(part_last, "fsdp", member, fsdp_bits)
    rows_at = member * tok_rows
    cols_at = section * piece_width
    dout_rows = lax.dynamic_slice_in_dim(dout_last, rows_at, tok_rows, axis=0)
    rows_last = rows_last + jnp.where(section == 0, dout_rows.astype(jnp.float32), 0.0)
    within = [rows_last] + [
        shifted(rows_last, "segment", k, sections) for k in range(1, sections)
    ]
    across = [
        lax.ppermute(
            rows_last, "segment", [(sections + sp, (sp + k) % sections) for sp in range(sections)]
        )
        for k in range(sections)
    ]
    grad_last = in_order(within, section, sections).astype(jnp.bfloat16)
    first_rows = jnp.where(
        is_last, grad_last, in_order(across, section, sections).astype(jnp.bfloat16)
    )
    dout_first = gather_any(first_rows, "fsdp", member, fsdp_bits).reshape(tokens, width)

    dout_sel = jnp.einsum("cr,trd->ctd", row_b, dout_first.reshape(tokens, nrow, blk))
    dout_sel = dout_sel.astype(jnp.bfloat16)
    dh_slot = jnp.einsum("ctd,chd->cth", dout_sel, w_down, preferred_element_type=jnp.float32)
    dh_part = jnp.einsum("cj,cth->tjh", col_f, dh_slot, precision=HOT)
    dh_part = dh_part.reshape(tokens, members, cols_per, blk).transpose(1, 0, 2, 3)
    dhidden_first = scatter_any(dh_part, "fsdp", member, fsdp_bits)
    dgate_first, dup_first = gate_grads(dhidden_first)
    shared_first = share([dgate_first, dup_first])
    cot_sel = jnp.where(
        is_last,
        jnp.einsum("cr,trd->ctd", row_b, dout_last.reshape(tokens, nrow, blk)).astype(
            jnp.bfloat16
        ),
        dout_sel,
    )
    hid_sel = jnp.einsum("cj,tjh->cth", col_b, hidden).astype(jnp.bfloat16)
    grad_down = jnp.einsum(
        "cth,ctd->chd", hid_sel, cot_sel, preferred_element_type=jnp.float32
    ).astype(jnp.bfloat16)
    zero_bf = jnp.zeros((), jnp.bfloat16)
    grad_down = jnp.where(valid[:, None, None], grad_down, zero_bf)
    grad_down, shared_first = lax.optimization_barrier((grad_down, shared_first))
    d_sel_first = select_pair(shared_first[0], shared_first[1])
    part_first = spread_rows(d_sel_first).reshape(members, tok_rows, width)
    part_first = scatter_any(part_first, "fsdp", member, fsdp_bits)
    part_first = part_first.reshape(tok_rows, sections, piece_width).transpose(1, 0, 2)
    part_first = scatter_any(part_first, "segment", section, sec_bits)

    own_last = lax.dynamic_slice_in_dim(grad_last, cols_at, piece_width, axis=1)
    own_dout = lax.dynamic_slice(dout_first, (rows_at, cols_at), (tok_rows, piece_width))
    grad_first = (own_dout.astype(jnp.float32) + part_first).astype(jnp.bfloat16)
    input_grads = jnp.where(is_last, own_last, grad_first)

    d_sel = jnp.where(is_last, d_sel_last, d_sel_first)
    x_pair = jnp.broadcast_to(x_sel[:, None], (capacity, 2, tokens, blk))
    grad_pair = jnp.einsum(
        "cgta,cgtb->cgab", x_pair, d_sel.transpose(0, 2, 1, 3),
        preferred_element_type=jnp.float32,
    ).astype(jnp.bfloat16)
    grad_pair = jnp.where(valid[:, None, None, None], grad_pair, zero_bf)
    return (input_grads, grad_pair[:, None], grad_down[:, None])


def solution(mesh):
    return jax.shard_map(
        per_device,
        mesh=mesh,
        in_specs=(
            P(("groups", "fsdp"), "segment"),
            P("groups"),
            P(),
            P("fsdp", "segment", None, None, None),
            P("fsdp", "segment", None, None),
            P(),
            P(),
            P(),
        ),
        out_specs=(
            P(("groups", "fsdp"), "segment"),
            P(("groups", "fsdp"), "segment", None, None, None),
            P(("groups", "fsdp"), "segment", None, None),
        ),
        check_vma=False,
    )
```

```python
import jax
import jax.numpy as jnp
from jax import lax
from jax.sharding import PartitionSpec as P

PIPE = 2
HI = lax.Precision.HIGHEST
HOT = lax.Precision.HIGH


def bits_of(size):
    return size.bit_length() - 1


def swapped(x, axis, bit):
    size = lax.axis_size(axis)
    return lax.ppermute(x, axis, [(i, i ^ (1 << bit)) for i in range(size)])


def all_sum(x, axis, levels):
    for bit in range(levels):
        x = x + swapped(x, axis, bit)
    return x


def gather_along(x, axis, index, levels, dim):
    for bit in range(levels):
        other = swapped(x, axis, bit)
        upper = (index >> bit) & 1 == 1
        x = jnp.where(
            upper,
            jnp.concatenate([other, x], axis=dim),
            jnp.concatenate([x, other], axis=dim),
        )
    return x


def scatter_along(x, axis, index, levels, dim):
    for bit in reversed(range(levels)):
        half = x.shape[dim] // 2
        upper = (index >> bit) & 1
        keep = lax.dynamic_slice_in_dim(x, upper * half, half, axis=dim)
        send = lax.dynamic_slice_in_dim(x, (1 - upper) * half, half, axis=dim)
        x = keep + swapped(send, axis, bit)
    return x


def scatter_blocks(x, axis, index, levels):
    x = x.reshape((2,) * levels + x.shape[1:])
    for bit in range(levels):
        pos = levels - 1 - bit
        mine = (index >> bit) & 1
        keep = lax.dynamic_index_in_dim(x, mine, pos, keepdims=False)
        send = lax.dynamic_index_in_dim(x, 1 - mine, pos, keepdims=False)
        x = keep + swapped(send, axis, bit)
    return x


def gather_blocks(x, axis, index, levels):
    for count, bit in enumerate(reversed(range(levels))):
        other = swapped(x, axis, bit)
        upper = (index >> bit) & 1 == 1
        x = jnp.where(
            upper, jnp.stack([other, x], axis=count), jnp.stack([x, other], axis=count)
        )
    return x.reshape((-1,) + x.shape[levels:])


DIRECT = 4


def shifted(x, axis, shift, group):
    size = lax.axis_size(axis)
    route = [(i, i - i % group + (i % group + shift) % group) for i in range(size)]
    return lax.ppermute(x, axis, route)


def scatter_any(x, axis, index, levels):
    n = 1 << levels
    if n > DIRECT:
        return scatter_blocks(x, axis, index, levels)
    total = lax.dynamic_index_in_dim(x, index, 0, keepdims=False)
    for shift in range(1, n):
        send = lax.dynamic_index_in_dim(x, (index + shift) % n, 0, keepdims=False)
        total = total + shifted(send, axis, shift, n)
    return total


def gather_any(x, axis, index, levels):
    n = 1 << levels
    if n > DIRECT:
        return gather_blocks(x, axis, index, levels)
    got = jnp.stack([x] + [shifted(x, axis, shift, n) for shift in range(1, n)])
    order = (index - jnp.arange(n, dtype=jnp.int32)) % n
    return jnp.take(got, order, axis=0)


def sum_any(x, axis, levels):
    n = 1 << levels
    if n > DIRECT:
        return all_sum(x, axis, levels)
    total = x
    for shift in range(1, n):
        total = total + shifted(x, axis, shift, n)
    return total


def per_device(
    layer_inputs, labels, head_weight, gate_up_store, down_store, kept_rows, owners, slots
):
    members = lax.axis_size("fsdp")
    places = lax.axis_size("segment")
    sections = places // PIPE
    member = lax.axis_index("fsdp")
    place = lax.axis_index("segment")
    segment = place // sections
    section = place % sections
    is_last = segment == PIPE - 1
    tok_rows, piece_width = layer_inputs.shape
    tokens = tok_rows * members
    width = piece_width * sections
    blk = gate_up_store.shape[-1]
    capacity = gate_up_store.shape[0]
    kept = kept_rows.shape[2]
    sec_cols = kept_rows.shape[1] // sections
    nrow = width // blk
    nblocks = sec_cols * kept

    first_col = section * sec_cols
    sec_rows = lax.dynamic_slice(kept_rows, (segment, first_col, 0), (1, sec_cols, kept))
    sec_owner = lax.dynamic_slice(owners, (segment, first_col, 0), (1, sec_cols, kept))
    sec_slot = lax.dynamic_slice(slots, (segment, first_col, 0), (1, sec_cols, kept))
    sec_rows = sec_rows.reshape(nblocks)
    mine = sec_owner.reshape(nblocks) == member
    block_col = jnp.arange(nblocks, dtype=jnp.int32) // kept
    hits = mine[None, :] & (
        sec_slot.reshape(nblocks)[None, :] == jnp.arange(capacity, dtype=jnp.int32)[:, None]
    )
    valid = jnp.any(hits, axis=1)
    slot_col = jnp.sum(jnp.where(hits, block_col[None, :], 0), axis=1)
    slot_row = jnp.sum(jnp.where(hits, sec_rows[None, :], 0), axis=1)
    col_hot = valid[:, None] & (slot_col[:, None] == jnp.arange(sec_cols, dtype=jnp.int32)[None, :])
    row_hot = valid[:, None] & (slot_row[:, None] == jnp.arange(nrow, dtype=jnp.int32)[None, :])
    col_f = col_hot.astype(jnp.float32)
    col_b = col_hot.astype(jnp.bfloat16)
    row_f = row_hot.astype(jnp.float32)
    row_b = row_hot.astype(jnp.bfloat16)

    w_pair = gate_up_store[:, 0]
    w_down = down_store[:, 0]

    fsdp_bits = bits_of(members)
    sec_bits = bits_of(sections)

    x_mine = gather_along(layer_inputs, "segment", section, sec_bits, 1)
    x_mine = gather_any(x_mine, "fsdp", member, fsdp_bits).reshape(tokens, width)
    x_sel = jnp.einsum("cr,trb->ctb", row_b, x_mine.reshape(tokens, nrow, blk))
    x_sel = x_sel.astype(jnp.bfloat16)

    gu_slot = jnp.einsum("cta,cgab->ctgb", x_sel, w_pair, preferred_element_type=jnp.float32)
    gu_part = jnp.einsum("cj,ctgb->gtjb", col_f, gu_slot, precision=HOT)
    head_rows = head_weight.reshape(nrow, blk)
    head_sel = jnp.einsum("cr,rd->cd", row_f, head_rows, precision=HI)
    head_hi = head_sel.astype(jnp.bfloat16)
    head_lo = (head_sel - head_hi.astype(jnp.float32)).astype(jnp.bfloat16)
    head_two = jnp.stack([head_hi, head_lo], axis=1)
    folded = jnp.einsum(
        "chd,ckd->chk", w_down, head_two, preferred_element_type=jnp.float32
    ).sum(axis=2)
    f_part = jnp.einsum("cj,ch->jh", col_f, folded, precision=HOT)
    cols_per = sec_cols // members
    packed = jnp.concatenate(
        [gu_part.reshape(2 * tokens, sec_cols, blk), f_part[None]], axis=0
    )
    packed = packed.reshape(2 * tokens + 1, members, cols_per, blk).transpose(1, 0, 2, 3)
    packed = scatter_any(packed, "fsdp", member, fsdp_bits)
    gate = packed[:tokens]
    up = packed[tokens:2 * tokens]
    f_sum = packed[2 * tokens]
    sig = jax.nn.sigmoid(gate)
    hidden_own = (gate * sig * up).astype(jnp.bfloat16)

    branch = jnp.einsum("tjh,jh->t", hidden_own.astype(jnp.float32), f_sum, precision=HI)
    x_term = jnp.einsum("td,d->t", x_mine.astype(jnp.float32), head_weight, precision=HI)
    branch = branch + jnp.where((section == 0) & (member == 0), x_term, 0.0)
    logits = sum_any(branch, "fsdp", fsdp_bits)
    logits = sum_any(logits, "segment", sec_bits) * width ** (-0.5)
    dlogit = jax.nn.sigmoid(logits) - labels.astype(jnp.float32)
    dout_last = (dlogit[:, None] * head_weight[None, :]).astype(jnp.bfloat16)

    def gate_grads(dhidden):
        dgate = (dhidden * up * sig * (1.0 + gate * (1.0 - sig))).astype(jnp.bfloat16)
        dup = (dhidden * gate * sig).astype(jnp.bfloat16)
        return dgate, dup

    def share(parts):
        whole = gather_any(jnp.stack(parts), "fsdp", member, fsdp_bits)
        n = len(parts)
        return whole.transpose(1, 2, 0, 3, 4).reshape(n, tokens, sec_cols, blk)

    def select_pair(dgate, dup):
        pair = jnp.stack([dgate, dup], axis=2)
        return jnp.einsum("cj,tjgb->ctgb", col_b, pair).astype(jnp.bfloat16)

    def spread_rows(d_sel):
        spread = jnp.einsum(
            "ctgb,cgab->cta", d_sel, w_pair, preferred_element_type=jnp.float32
        )
        return jnp.einsum("cr,cta->tra", row_f, spread, precision=HOT).reshape(tokens, width)

    dgate_last, dup_last = gate_grads(dlogit[:, None, None] * f_sum[None])
    shared = share([hidden_own, dgate_last, dup_last])
    hidden = shared[0]
    d_sel_last = select_pair(shared[1], shared[2])
    sum_last = all_sum(spread_rows(d_sel_last), "fsdp", fsdp_bits)
    sum_last = sum_any(sum_last, "segment", sec_bits)
    grad_all = (dout_last.astype(jnp.float32) + sum_last).astype(jnp.bfloat16)
    handed = lax.ppermute(
        grad_all, "segment", [(i, i - sections) for i in range(sections, places)]
    )
    dout_first = jnp.where(is_last, grad_all, handed)
    rows_at = member * tok_rows
    cols_at = section * piece_width

    dout_sel = jnp.einsum("cr,trd->ctd", row_b, dout_first.reshape(tokens, nrow, blk))
    dout_sel = dout_sel.astype(jnp.bfloat16)
    dh_slot = jnp.einsum("ctd,chd->cth", dout_sel, w_down, preferred_element_type=jnp.float32)
    dh_part = jnp.einsum("cj,cth->tjh", col_f, dh_slot, precision=HOT)
    dh_part = dh_part.reshape(tokens, members, cols_per, blk).transpose(1, 0, 2, 3)
    dhidden_first = scatter_any(dh_part, "fsdp", member, fsdp_bits)
    dgate_first, dup_first = gate_grads(dhidden_first)
    shared_first = share([dgate_first, dup_first])
    cot_sel = jnp.where(
        is_last,
        jnp.einsum("cr,trd->ctd", row_b, dout_last.reshape(tokens, nrow, blk)).astype(
            jnp.bfloat16
        ),
        dout_sel,
    )
    hid_sel = jnp.einsum("cj,tjh->cth", col_b, hidden).astype(jnp.bfloat16)
    grad_down = jnp.einsum(
        "cth,ctd->chd", hid_sel, cot_sel, preferred_element_type=jnp.float32
    ).astype(jnp.bfloat16)
    zero_bf = jnp.zeros((), jnp.bfloat16)
    grad_down = jnp.where(valid[:, None, None], grad_down, zero_bf)
    grad_down, shared_first = lax.optimization_barrier((grad_down, shared_first))
    d_sel_first = select_pair(shared_first[0], shared_first[1])
    part_first = spread_rows(d_sel_first).reshape(members, tok_rows, width)
    part_first = scatter_any(part_first, "fsdp", member, fsdp_bits)
    part_first = part_first.reshape(tok_rows, sections, piece_width).transpose(1, 0, 2)
    part_first = scatter_any(part_first, "segment", section, sec_bits)

    own_last = lax.dynamic_slice(grad_all, (rows_at, cols_at), (tok_rows, piece_width))
    own_dout = lax.dynamic_slice(dout_first, (rows_at, cols_at), (tok_rows, piece_width))
    grad_first = (own_dout.astype(jnp.float32) + part_first).astype(jnp.bfloat16)
    input_grads = jnp.where(is_last, own_last, grad_first)

    d_sel = jnp.where(is_last, d_sel_last, d_sel_first)
    x_pair = jnp.broadcast_to(x_sel[:, None], (capacity, 2, tokens, blk))
    grad_pair = jnp.einsum(
        "cgta,cgtb->cgab", x_pair, d_sel.transpose(0, 2, 1, 3),
        preferred_element_type=jnp.float32,
    ).astype(jnp.bfloat16)
    grad_pair = jnp.where(valid[:, None, None, None], grad_pair, zero_bf)
    return (input_grads, grad_pair[:, None], grad_down[:, None])


def solution(mesh):
    return jax.shard_map(
        per_device,
        mesh=mesh,
        in_specs=(
            P(("groups", "fsdp"), "segment"),
            P("groups"),
            P(),
            P("fsdp", "segment", None, None, None),
            P("fsdp", "segment", None, None),
            P(),
            P(),
            P(),
        ),
        out_specs=(
            P(("groups", "fsdp"), "segment"),
            P(("groups", "fsdp"), "segment", None, None, None),
            P(("groups", "fsdp"), "segment", None, None),
        ),
        check_vma=False,
    )
```

```python
import jax
import jax.numpy as jnp
from jax import lax
from jax.sharding import PartitionSpec as P

PIPE = 2
HI = lax.Precision.HIGHEST
HOT = lax.Precision.HIGH


def bits_of(size):
    return size.bit_length() - 1


def swapped(x, axis, bit):
    size = lax.axis_size(axis)
    return lax.ppermute(x, axis, [(i, i ^ (1 << bit)) for i in range(size)])


def all_sum(x, axis, levels):
    for bit in range(levels):
        x = x + swapped(x, axis, bit)
    return x


def gather_along(x, axis, index, levels, dim):
    for bit in range(levels):
        other = swapped(x, axis, bit)
        upper = (index >> bit) & 1 == 1
        x = jnp.where(
            upper,
            jnp.concatenate([other, x], axis=dim),
            jnp.concatenate([x, other], axis=dim),
        )
    return x


def scatter_along(x, axis, index, levels, dim):
    for bit in reversed(range(levels)):
        half = x.shape[dim] // 2
        upper = (index >> bit) & 1
        keep = lax.dynamic_slice_in_dim(x, upper * half, half, axis=dim)
        send = lax.dynamic_slice_in_dim(x, (1 - upper) * half, half, axis=dim)
        x = keep + swapped(send, axis, bit)
    return x


def scatter_blocks(x, axis, index, levels):
    x = x.reshape((2,) * levels + x.shape[1:])
    for bit in range(levels):
        pos = levels - 1 - bit
        mine = (index >> bit) & 1
        keep = lax.dynamic_index_in_dim(x, mine, pos, keepdims=False)
        send = lax.dynamic_index_in_dim(x, 1 - mine, pos, keepdims=False)
        x = keep + swapped(send, axis, bit)
    return x


def gather_blocks(x, axis, index, levels):
    for count, bit in enumerate(reversed(range(levels))):
        other = swapped(x, axis, bit)
        upper = (index >> bit) & 1 == 1
        x = jnp.where(
            upper, jnp.stack([other, x], axis=count), jnp.stack([x, other], axis=count)
        )
    return x.reshape((-1,) + x.shape[levels:])


DIRECT = 4


def shifted(x, axis, shift, group):
    size = lax.axis_size(axis)
    route = [(i, i - i % group + (i % group + shift) % group) for i in range(size)]
    return lax.ppermute(x, axis, route)


def scatter_any(x, axis, index, levels):
    n = 1 << levels
    if n > DIRECT:
        return scatter_blocks(x, axis, index, levels)
    total = lax.dynamic_index_in_dim(x, index, 0, keepdims=False)
    for shift in range(1, n):
        send = lax.dynamic_index_in_dim(x, (index + shift) % n, 0, keepdims=False)
        total = total + shifted(send, axis, shift, n)
    return total


def gather_any(x, axis, index, levels):
    n = 1 << levels
    if n > DIRECT:
        return gather_blocks(x, axis, index, levels)
    got = jnp.stack([x] + [shifted(x, axis, shift, n) for shift in range(1, n)])
    order = (index - jnp.arange(n, dtype=jnp.int32)) % n
    return jnp.take(got, order, axis=0)


def sum_any(x, axis, levels):
    n = 1 << levels
    if n > DIRECT:
        return all_sum(x, axis, levels)
    total = x
    for shift in range(1, n):
        total = total + shifted(x, axis, shift, n)
    return total


def per_device(
    layer_inputs, labels, head_weight, gate_up_store, down_store, kept_rows, owners, slots
):
    members = lax.axis_size("fsdp")
    places = lax.axis_size("segment")
    sections = places // PIPE
    member = lax.axis_index("fsdp")
    place = lax.axis_index("segment")
    segment = place // sections
    section = place % sections
    is_last = segment == PIPE - 1
    tok_rows, piece_width = layer_inputs.shape
    tokens = tok_rows * members
    width = piece_width * sections
    blk = gate_up_store.shape[-1]
    capacity = gate_up_store.shape[0]
    kept = kept_rows.shape[2]
    sec_cols = kept_rows.shape[1] // sections
    nrow = width // blk
    nblocks = sec_cols * kept

    first_col = section * sec_cols
    sec_rows = lax.dynamic_slice(kept_rows, (segment, first_col, 0), (1, sec_cols, kept))
    sec_owner = lax.dynamic_slice(owners, (segment, first_col, 0), (1, sec_cols, kept))
    sec_slot = lax.dynamic_slice(slots, (segment, first_col, 0), (1, sec_cols, kept))
    sec_rows = sec_rows.reshape(nblocks)
    mine = sec_owner.reshape(nblocks) == member
    block_col = jnp.arange(nblocks, dtype=jnp.int32) // kept
    hits = mine[None, :] & (
        sec_slot.reshape(nblocks)[None, :] == jnp.arange(capacity, dtype=jnp.int32)[:, None]
    )
    valid = jnp.any(hits, axis=1)
    slot_col = jnp.sum(jnp.where(hits, block_col[None, :], 0), axis=1)
    slot_row = jnp.sum(jnp.where(hits, sec_rows[None, :], 0), axis=1)
    col_hot = valid[:, None] & (slot_col[:, None] == jnp.arange(sec_cols, dtype=jnp.int32)[None, :])
    row_hot = valid[:, None] & (slot_row[:, None] == jnp.arange(nrow, dtype=jnp.int32)[None, :])
    col_f = col_hot.astype(jnp.float32)
    col_b = col_hot.astype(jnp.bfloat16)
    row_f = row_hot.astype(jnp.float32)
    row_b = row_hot.astype(jnp.bfloat16)

    w_pair = gate_up_store[:, 0]
    w_down = down_store[:, 0]

    fsdp_bits = bits_of(members)
    sec_bits = bits_of(sections)

    x_mine = gather_along(layer_inputs, "segment", section, sec_bits, 1)
    x_mine = gather_any(x_mine, "fsdp", member, fsdp_bits).reshape(tokens, width)
    x_sel = jnp.einsum("cr,trb->ctb", row_b, x_mine.reshape(tokens, nrow, blk))
    x_sel = x_sel.astype(jnp.bfloat16)

    gu_slot = jnp.einsum("cta,cgab->ctgb", x_sel, w_pair, preferred_element_type=jnp.float32)
    gu_part = jnp.einsum("cj,ctgb->gtjb", col_f, gu_slot, precision=HOT)
    head_rows = head_weight.reshape(nrow, blk)
    head_sel = jnp.einsum("cr,rd->cd", row_f, head_rows, precision=HI)
    head_hi = head_sel.astype(jnp.bfloat16)
    head_lo = (head_sel - head_hi.astype(jnp.float32)).astype(jnp.bfloat16)
    head_two = jnp.stack([head_hi, head_lo], axis=1)
    folded = jnp.einsum(
        "chd,ckd->chk", w_down, head_two, preferred_element_type=jnp.float32
    ).sum(axis=2)
    f_part = jnp.einsum("cj,ch->jh", col_f, folded, precision=HOT)
    cols_per = sec_cols // members
    packed = jnp.concatenate(
        [gu_part.reshape(2 * tokens, sec_cols, blk), f_part[None]], axis=0
    )
    packed = packed.reshape(2 * tokens + 1, members, cols_per, blk).transpose(1, 0, 2, 3)
    packed = scatter_any(packed, "fsdp", member, fsdp_bits)
    gate = packed[:tokens]
    up = packed[tokens:2 * tokens]
    f_sum = packed[2 * tokens]
    sig = jax.nn.sigmoid(gate)
    hidden_own = (gate * sig * up).astype(jnp.bfloat16)

    branch = jnp.einsum("tjh,jh->t", hidden_own.astype(jnp.float32), f_sum, precision=HI)
    x_term = jnp.einsum("td,d->t", x_mine.astype(jnp.float32), head_weight, precision=HI)
    branch = branch + jnp.where((section == 0) & (member == 0), x_term, 0.0)
    logits = sum_any(branch, "fsdp", fsdp_bits)
    logits = sum_any(logits, "segment", sec_bits) * width ** (-0.5)
    dlogit = jax.nn.sigmoid(logits) - labels.astype(jnp.float32)
    dout_last = (dlogit[:, None] * head_weight[None, :]).astype(jnp.bfloat16)

    def gate_grads(dhidden):
        dgate = (dhidden * up * sig * (1.0 + gate * (1.0 - sig))).astype(jnp.bfloat16)
        dup = (dhidden * gate * sig).astype(jnp.bfloat16)
        return dgate, dup

    def share(parts):
        whole = gather_any(jnp.stack(parts), "fsdp", member, fsdp_bits)
        n = len(parts)
        return whole.transpose(1, 2, 0, 3, 4).reshape(n, tokens, sec_cols, blk)

    def select_pair(dgate, dup):
        pair = jnp.stack([dgate, dup], axis=2)
        return jnp.einsum("cj,tjgb->ctgb", col_b, pair).astype(jnp.bfloat16)

    def spread_rows(d_sel):
        spread = jnp.einsum(
            "ctgb,cgab->cta", d_sel, w_pair, preferred_element_type=jnp.float32
        )
        return jnp.einsum("cr,cta->tra", row_f, spread, precision=HOT).reshape(tokens, width)

    dgate_last, dup_last = gate_grads(dlogit[:, None, None] * f_sum[None])
    shared = share([hidden_own, dgate_last, dup_last])
    hidden = shared[0]
    d_sel_last = select_pair(shared[1], shared[2])
    sum_last = all_sum(spread_rows(d_sel_last), "fsdp", fsdp_bits)
    sum_last = sum_any(sum_last, "segment", sec_bits)
    grad_all = (dout_last.astype(jnp.float32) + sum_last).astype(jnp.bfloat16)
    handed = lax.ppermute(
        grad_all, "segment", [(i, i - sections) for i in range(sections, places)]
    )
    dout_first = jnp.where(is_last, grad_all, handed)
    rows_at = member * tok_rows
    cols_at = section * piece_width

    dout_sel = jnp.einsum("cr,trd->ctd", row_b, dout_first.reshape(tokens, nrow, blk))
    dout_sel = dout_sel.astype(jnp.bfloat16)
    dh_slot = jnp.einsum("ctd,chd->cth", dout_sel, w_down, preferred_element_type=jnp.float32)
    dh_part = jnp.einsum("cj,cth->tjh", col_f, dh_slot, precision=HOT)
    dh_part = dh_part.reshape(tokens, members, cols_per, blk).transpose(1, 0, 2, 3)
    dhidden_first = scatter_any(dh_part, "fsdp", member, fsdp_bits)
    dgate_first, dup_first = gate_grads(dhidden_first)
    shared_first = share([dgate_first, dup_first])
    cot_sel = jnp.where(
        is_last,
        jnp.einsum("cr,trd->ctd", row_b, dout_last.reshape(tokens, nrow, blk)).astype(
            jnp.bfloat16
        ),
        dout_sel,
    )
    hid_sel = jnp.einsum("cj,tjh->cth", col_b, hidden).astype(jnp.bfloat16)
    grad_down = jnp.einsum(
        "cth,ctd->chd", hid_sel, cot_sel, preferred_element_type=jnp.float32
    ).astype(jnp.bfloat16)
    grad_down, shared_first = lax.optimization_barrier((grad_down, shared_first))
    d_sel_first = select_pair(shared_first[0], shared_first[1])
    part_first = spread_rows(d_sel_first).reshape(members, tok_rows, width)
    part_first = scatter_any(part_first, "fsdp", member, fsdp_bits)
    part_first = part_first.reshape(tok_rows, sections, piece_width).transpose(1, 0, 2)
    part_first = scatter_any(part_first, "segment", section, sec_bits)

    own_last = lax.dynamic_slice(grad_all, (rows_at, cols_at), (tok_rows, piece_width))
    own_dout = lax.dynamic_slice(dout_first, (rows_at, cols_at), (tok_rows, piece_width))
    grad_first = (own_dout.astype(jnp.float32) + part_first).astype(jnp.bfloat16)
    input_grads = jnp.where(is_last, own_last, grad_first)

    d_sel = jnp.where(is_last, d_sel_last, d_sel_first)
    x_pair = jnp.broadcast_to(x_sel[:, None], (capacity, 2, tokens, blk))
    grad_pair = jnp.einsum(
        "cgta,cgtb->cgab", x_pair, d_sel.transpose(0, 2, 1, 3),
        preferred_element_type=jnp.float32,
    ).astype(jnp.bfloat16)
    return (input_grads, grad_pair[:, None], grad_down[:, None])


def solution(mesh):
    return jax.shard_map(
        per_device,
        mesh=mesh,
        in_specs=(
            P(("groups", "fsdp"), "segment"),
            P("groups"),
            P(),
            P("fsdp", "segment", None, None, None),
            P("fsdp", "segment", None, None),
            P(),
            P(),
            P(),
        ),
        out_specs=(
            P(("groups", "fsdp"), "segment"),
            P(("groups", "fsdp"), "segment", None, None, None),
            P(("groups", "fsdp"), "segment", None, None),
        ),
        check_vma=False,
    )
```

```python
import jax
import jax.numpy as jnp
from jax import lax
from jax.sharding import PartitionSpec as P

PIPE = 2
HI = lax.Precision.HIGHEST
HOT = lax.Precision.HIGH


def bits_of(size):
    return size.bit_length() - 1


def swapped(x, axis, bit):
    size = lax.axis_size(axis)
    return lax.ppermute(x, axis, [(i, i ^ (1 << bit)) for i in range(size)])


def all_sum(x, axis, levels):
    for bit in range(levels):
        x = x + swapped(x, axis, bit)
    return x


def gather_along(x, axis, index, levels, dim):
    for bit in range(levels):
        other = swapped(x, axis, bit)
        upper = (index >> bit) & 1 == 1
        x = jnp.where(
            upper,
            jnp.concatenate([other, x], axis=dim),
            jnp.concatenate([x, other], axis=dim),
        )
    return x


def scatter_along(x, axis, index, levels, dim):
    for bit in reversed(range(levels)):
        half = x.shape[dim] // 2
        upper = (index >> bit) & 1
        keep = lax.dynamic_slice_in_dim(x, upper * half, half, axis=dim)
        send = lax.dynamic_slice_in_dim(x, (1 - upper) * half, half, axis=dim)
        x = keep + swapped(send, axis, bit)
    return x


def scatter_blocks(x, axis, index, levels):
    x = x.reshape((2,) * levels + x.shape[1:])
    for bit in range(levels):
        pos = levels - 1 - bit
        mine = (index >> bit) & 1
        keep = lax.dynamic_index_in_dim(x, mine, pos, keepdims=False)
        send = lax.dynamic_index_in_dim(x, 1 - mine, pos, keepdims=False)
        x = keep + swapped(send, axis, bit)
    return x


def gather_blocks(x, axis, index, levels):
    for count, bit in enumerate(reversed(range(levels))):
        other = swapped(x, axis, bit)
        upper = (index >> bit) & 1 == 1
        x = jnp.where(
            upper, jnp.stack([other, x], axis=count), jnp.stack([x, other], axis=count)
        )
    return x.reshape((-1,) + x.shape[levels:])


DIRECT = 4


def shifted(x, axis, shift, group):
    size = lax.axis_size(axis)
    route = [(i, i - i % group + (i % group + shift) % group) for i in range(size)]
    return lax.ppermute(x, axis, route)


def scatter_any(x, axis, index, levels):
    n = 1 << levels
    if n > DIRECT:
        return scatter_blocks(x, axis, index, levels)
    total = lax.dynamic_index_in_dim(x, index, 0, keepdims=False)
    for shift in range(1, n):
        send = lax.dynamic_index_in_dim(x, (index + shift) % n, 0, keepdims=False)
        total = total + shifted(send, axis, shift, n)
    return total


def gather_any(x, axis, index, levels):
    n = 1 << levels
    if n > DIRECT:
        return gather_blocks(x, axis, index, levels)
    got = jnp.stack([x] + [shifted(x, axis, shift, n) for shift in range(1, n)])
    order = (index - jnp.arange(n, dtype=jnp.int32)) % n
    return jnp.take(got, order, axis=0)


def sum_any(x, axis, levels):
    n = 1 << levels
    if n > DIRECT:
        return all_sum(x, axis, levels)
    total = x
    for shift in range(1, n):
        total = total + shifted(x, axis, shift, n)
    return total


def per_device(
    layer_inputs, labels, head_weight, gate_up_store, down_store, kept_rows, owners, slots
):
    members = lax.axis_size("fsdp")
    places = lax.axis_size("segment")
    sections = places // PIPE
    member = lax.axis_index("fsdp")
    place = lax.axis_index("segment")
    segment = place // sections
    section = place % sections
    is_last = segment == PIPE - 1
    tok_rows, piece_width = layer_inputs.shape
    tokens = tok_rows * members
    width = piece_width * sections
    blk = gate_up_store.shape[-1]
    capacity = gate_up_store.shape[0]
    kept = kept_rows.shape[2]
    sec_cols = kept_rows.shape[1] // sections
    nrow = width // blk
    nblocks = sec_cols * kept

    first_col = section * sec_cols
    sec_rows = lax.dynamic_slice(kept_rows, (segment, first_col, 0), (1, sec_cols, kept))
    sec_owner = lax.dynamic_slice(owners, (segment, first_col, 0), (1, sec_cols, kept))
    sec_slot = lax.dynamic_slice(slots, (segment, first_col, 0), (1, sec_cols, kept))
    sec_rows = sec_rows.reshape(nblocks)
    mine = sec_owner.reshape(nblocks) == member
    block_col = jnp.arange(nblocks, dtype=jnp.int32) // kept
    hits = mine[None, :] & (
        sec_slot.reshape(nblocks)[None, :] == jnp.arange(capacity, dtype=jnp.int32)[:, None]
    )
    valid = jnp.any(hits, axis=1)
    slot_col = jnp.sum(jnp.where(hits, block_col[None, :], 0), axis=1)
    slot_row = jnp.sum(jnp.where(hits, sec_rows[None, :], 0), axis=1)
    col_hot = valid[:, None] & (slot_col[:, None] == jnp.arange(sec_cols, dtype=jnp.int32)[None, :])
    row_hot = valid[:, None] & (slot_row[:, None] == jnp.arange(nrow, dtype=jnp.int32)[None, :])
    col_f = col_hot.astype(jnp.float32)
    col_b = col_hot.astype(jnp.bfloat16)
    row_f = row_hot.astype(jnp.float32)
    row_b = row_hot.astype(jnp.bfloat16)

    w_pair = gate_up_store[:, 0]
    w_down = down_store[:, 0]

    fsdp_bits = bits_of(members)
    sec_bits = bits_of(sections)

    x_mine = gather_along(layer_inputs, "segment", section, sec_bits, 1)
    head_sel = jnp.einsum("cr,rd->cd", row_f, head_weight.reshape(nrow, blk), precision=HI)
    x_mine, head_sel = lax.optimization_barrier((x_mine, head_sel))
    x_mine = gather_any(x_mine, "fsdp", member, fsdp_bits).reshape(tokens, width)
    x_sel = jnp.einsum("cr,trb->ctb", row_b, x_mine.reshape(tokens, nrow, blk))
    x_sel = x_sel.astype(jnp.bfloat16)

    gu_slot = jnp.einsum("cta,cgab->ctgb", x_sel, w_pair, preferred_element_type=jnp.float32)
    gu_part = jnp.einsum("cj,ctgb->gtjb", col_f, gu_slot, precision=HOT)
    head_hi = head_sel.astype(jnp.bfloat16)
    head_lo = (head_sel - head_hi.astype(jnp.float32)).astype(jnp.bfloat16)
    head_two = jnp.stack([head_hi, head_lo], axis=1)
    folded = jnp.einsum(
        "chd,ckd->chk", w_down, head_two, preferred_element_type=jnp.float32
    ).sum(axis=2)
    f_part = jnp.einsum("cj,ch->jh", col_f, folded, precision=HOT)
    cols_per = sec_cols // members
    packed = gu_part.reshape(2 * tokens, members, cols_per, blk).transpose(1, 0, 2, 3)
    packed = scatter_any(packed, "fsdp", member, fsdp_bits)
    gate = packed[:tokens]
    up = packed[tokens:]
    f_sum = scatter_any(f_part.reshape(members, cols_per, blk), "fsdp", member, fsdp_bits)
    sig = jax.nn.sigmoid(gate)
    hidden_own = (gate * sig * up).astype(jnp.bfloat16)

    branch = jnp.einsum("tjh,jh->t", hidden_own.astype(jnp.float32), f_sum, precision=HI)
    x_term = jnp.einsum("td,d->t", x_mine.astype(jnp.float32), head_weight, precision=HI)
    branch = branch + jnp.where((section == 0) & (member == 0), x_term, 0.0)
    logits = sum_any(branch, "fsdp", fsdp_bits)
    logits = sum_any(logits, "segment", sec_bits) * width ** (-0.5)
    dlogit = jax.nn.sigmoid(logits) - labels.astype(jnp.float32)
    dout_last = (dlogit[:, None] * head_weight[None, :]).astype(jnp.bfloat16)

    def gate_grads(dhidden):
        dgate = (dhidden * up * sig * (1.0 + gate * (1.0 - sig))).astype(jnp.bfloat16)
        dup = (dhidden * gate * sig).astype(jnp.bfloat16)
        return dgate, dup

    def share(parts):
        whole = gather_any(jnp.stack(parts), "fsdp", member, fsdp_bits)
        n = len(parts)
        return whole.transpose(1, 2, 0, 3, 4).reshape(n, tokens, sec_cols, blk)

    def select_pair(dgate, dup):
        pair = jnp.stack([dgate, dup], axis=2)
        return jnp.einsum("cj,tjgb->ctgb", col_b, pair).astype(jnp.bfloat16)

    def spread_rows(d_sel):
        spread = jnp.einsum(
            "ctgb,cgab->cta", d_sel, w_pair, preferred_element_type=jnp.float32
        )
        return jnp.einsum("cr,cta->tra", row_f, spread, precision=HOT).reshape(tokens, width)

    dgate_last, dup_last = gate_grads(dlogit[:, None, None] * f_sum[None])
    shared = share([hidden_own, dgate_last, dup_last])
    hidden = shared[0]
    d_sel_last = select_pair(shared[1], shared[2])
    part_last = spread_rows(d_sel_last).reshape(members, tok_rows, width)
    rows_last = scatter_any(part_last, "fsdp", member, fsdp_bits)
    rows_last = sum_any(rows_last, "segment", sec_bits)
    rows_at = member * tok_rows
    cols_at = section * piece_width
    dout_rows = lax.dynamic_slice_in_dim(dout_last, rows_at, tok_rows, axis=0)
    grad_last = (dout_rows.astype(jnp.float32) + rows_last).astype(jnp.bfloat16)
    handed = lax.ppermute(
        grad_last, "segment", [(i, i - sections) for i in range(sections, places)]
    )
    first_rows = jnp.where(is_last, grad_last, handed)
    dout_first = gather_any(first_rows, "fsdp", member, fsdp_bits).reshape(tokens, width)

    dout_sel = jnp.einsum("cr,trd->ctd", row_b, dout_first.reshape(tokens, nrow, blk))
    dout_sel = dout_sel.astype(jnp.bfloat16)
    dh_slot = jnp.einsum("ctd,chd->cth", dout_sel, w_down, preferred_element_type=jnp.float32)
    dh_part = jnp.einsum("cj,cth->tjh", col_f, dh_slot, precision=HOT)
    dh_part = dh_part.reshape(tokens, members, cols_per, blk).transpose(1, 0, 2, 3)
    dhidden_first = scatter_any(dh_part, "fsdp", member, fsdp_bits)
    dgate_first, dup_first = gate_grads(dhidden_first)
    shared_first = share([dgate_first, dup_first])
    cot_sel = jnp.where(
        is_last,
        jnp.einsum("cr,trd->ctd", row_b, dout_last.reshape(tokens, nrow, blk)).astype(
            jnp.bfloat16
        ),
        dout_sel,
    )
    hid_sel = jnp.einsum("cj,tjh->cth", col_b, hidden).astype(jnp.bfloat16)
    grad_down = jnp.einsum(
        "cth,ctd->chd", hid_sel, cot_sel, preferred_element_type=jnp.float32
    ).astype(jnp.bfloat16)
    zero_bf = jnp.zeros((), jnp.bfloat16)
    grad_down = jnp.where(valid[:, None, None], grad_down, zero_bf)
    grad_down, shared_first = lax.optimization_barrier((grad_down, shared_first))
    d_sel_first = select_pair(shared_first[0], shared_first[1])
    part_first = spread_rows(d_sel_first).reshape(members, tok_rows, width)
    part_first = scatter_any(part_first, "fsdp", member, fsdp_bits)
    part_first = part_first.reshape(tok_rows, sections, piece_width).transpose(1, 0, 2)
    part_first = scatter_any(part_first, "segment", section, sec_bits)

    own_last = lax.dynamic_slice_in_dim(grad_last, cols_at, piece_width, axis=1)
    own_dout = lax.dynamic_slice(dout_first, (rows_at, cols_at), (tok_rows, piece_width))
    grad_first = (own_dout.astype(jnp.float32) + part_first).astype(jnp.bfloat16)
    input_grads = jnp.where(is_last, own_last, grad_first)

    d_sel = jnp.where(is_last, d_sel_last, d_sel_first)
    x_pair = jnp.broadcast_to(x_sel[:, None], (capacity, 2, tokens, blk))
    grad_pair = jnp.einsum(
        "cgta,cgtb->cgab", x_pair, d_sel.transpose(0, 2, 1, 3),
        preferred_element_type=jnp.float32,
    ).astype(jnp.bfloat16)
    grad_pair = jnp.where(valid[:, None, None, None], grad_pair, zero_bf)
    return (input_grads, grad_pair[:, None], grad_down[:, None])


def solution(mesh):
    return jax.shard_map(
        per_device,
        mesh=mesh,
        in_specs=(
            P(("groups", "fsdp"), "segment"),
            P("groups"),
            P(),
            P("fsdp", "segment", None, None, None),
            P("fsdp", "segment", None, None),
            P(),
            P(),
            P(),
        ),
        out_specs=(
            P(("groups", "fsdp"), "segment"),
            P(("groups", "fsdp"), "segment", None, None, None),
            P(("groups", "fsdp"), "segment", None, None),
        ),
        check_vma=False,
    )
```

```python
import jax
import jax.numpy as jnp
from jax import lax
from jax.sharding import PartitionSpec as P

PIPE = 2
HI = lax.Precision.HIGHEST
HOT = lax.Precision.HIGH


def bits_of(size):
    return size.bit_length() - 1


def swapped(x, axis, bit):
    size = lax.axis_size(axis)
    return lax.ppermute(x, axis, [(i, i ^ (1 << bit)) for i in range(size)])


def all_sum(x, axis, levels):
    for bit in range(levels):
        x = x + swapped(x, axis, bit)
    return x


def gather_along(x, axis, index, levels, dim):
    for bit in range(levels):
        other = swapped(x, axis, bit)
        upper = (index >> bit) & 1 == 1
        x = jnp.where(
            upper,
            jnp.concatenate([other, x], axis=dim),
            jnp.concatenate([x, other], axis=dim),
        )
    return x


def scatter_along(x, axis, index, levels, dim):
    for bit in reversed(range(levels)):
        half = x.shape[dim] // 2
        upper = (index >> bit) & 1
        keep = lax.dynamic_slice_in_dim(x, upper * half, half, axis=dim)
        send = lax.dynamic_slice_in_dim(x, (1 - upper) * half, half, axis=dim)
        x = keep + swapped(send, axis, bit)
    return x


def scatter_blocks(x, axis, index, levels):
    x = x.reshape((2,) * levels + x.shape[1:])
    for bit in range(levels):
        pos = levels - 1 - bit
        mine = (index >> bit) & 1
        keep = lax.dynamic_index_in_dim(x, mine, pos, keepdims=False)
        send = lax.dynamic_index_in_dim(x, 1 - mine, pos, keepdims=False)
        x = keep + swapped(send, axis, bit)
    return x


def gather_blocks(x, axis, index, levels):
    for count, bit in enumerate(reversed(range(levels))):
        other = swapped(x, axis, bit)
        upper = (index >> bit) & 1 == 1
        x = jnp.where(
            upper, jnp.stack([other, x], axis=count), jnp.stack([x, other], axis=count)
        )
    return x.reshape((-1,) + x.shape[levels:])


DIRECT = 4


def shifted(x, axis, shift, group):
    size = lax.axis_size(axis)
    route = [(i, i - i % group + (i % group + shift) % group) for i in range(size)]
    return lax.ppermute(x, axis, route)


def scatter_any(x, axis, index, levels):
    n = 1 << levels
    if n > DIRECT:
        return scatter_blocks(x, axis, index, levels)
    total = lax.dynamic_index_in_dim(x, index, 0, keepdims=False)
    for shift in range(1, n):
        send = lax.dynamic_index_in_dim(x, (index + shift) % n, 0, keepdims=False)
        total = total + shifted(send, axis, shift, n)
    return total


def gather_any(x, axis, index, levels):
    n = 1 << levels
    if n > DIRECT:
        return gather_blocks(x, axis, index, levels)
    got = jnp.stack([x] + [shifted(x, axis, shift, n) for shift in range(1, n)])
    order = (index - jnp.arange(n, dtype=jnp.int32)) % n
    return jnp.take(got, order, axis=0)


def sum_any(x, axis, levels):
    n = 1 << levels
    if n > DIRECT:
        return all_sum(x, axis, levels)
    total = x
    for shift in range(1, n):
        total = total + shifted(x, axis, shift, n)
    return total


def per_device(
    layer_inputs, labels, head_weight, gate_up_store, down_store, kept_rows, owners, slots
):
    members = lax.axis_size("fsdp")
    places = lax.axis_size("segment")
    sections = places // PIPE
    member = lax.axis_index("fsdp")
    place = lax.axis_index("segment")
    segment = place // sections
    section = place % sections
    is_last = segment == PIPE - 1
    tok_rows, piece_width = layer_inputs.shape
    tokens = tok_rows * members
    width = piece_width * sections
    blk = gate_up_store.shape[-1]
    capacity = gate_up_store.shape[0]
    kept = kept_rows.shape[2]
    sec_cols = kept_rows.shape[1] // sections
    nrow = width // blk
    nblocks = sec_cols * kept

    first_col = section * sec_cols
    sec_rows = lax.dynamic_slice(kept_rows, (segment, first_col, 0), (1, sec_cols, kept))
    sec_owner = lax.dynamic_slice(owners, (segment, first_col, 0), (1, sec_cols, kept))
    sec_slot = lax.dynamic_slice(slots, (segment, first_col, 0), (1, sec_cols, kept))
    sec_rows = sec_rows.reshape(nblocks)
    mine = sec_owner.reshape(nblocks) == member
    block_col = jnp.arange(nblocks, dtype=jnp.int32) // kept
    hits = mine[None, :] & (
        sec_slot.reshape(nblocks)[None, :] == jnp.arange(capacity, dtype=jnp.int32)[:, None]
    )
    valid = jnp.any(hits, axis=1)
    slot_col = jnp.sum(jnp.where(hits, block_col[None, :], 0), axis=1)
    slot_row = jnp.sum(jnp.where(hits, sec_rows[None, :], 0), axis=1)
    col_hot = valid[:, None] & (slot_col[:, None] == jnp.arange(sec_cols, dtype=jnp.int32)[None, :])
    row_hot = valid[:, None] & (slot_row[:, None] == jnp.arange(nrow, dtype=jnp.int32)[None, :])
    col_f = col_hot.astype(jnp.float32)
    col_b = col_hot.astype(jnp.bfloat16)
    row_f = row_hot.astype(jnp.float32)
    row_b = row_hot.astype(jnp.bfloat16)

    w_pair = gate_up_store[:, 0]
    w_down = down_store[:, 0]

    fsdp_bits = bits_of(members)
    sec_bits = bits_of(sections)

    x_mine = gather_along(layer_inputs, "segment", section, sec_bits, 1)
    head_sel = jnp.einsum("cr,rd->cd", row_f, head_weight.reshape(nrow, blk), precision=HI)
    x_mine, head_sel = lax.optimization_barrier((x_mine, head_sel))
    x_mine = gather_any(x_mine, "fsdp", member, fsdp_bits).reshape(tokens, width)
    x_sel = jnp.einsum("cr,trb->ctb", row_b, x_mine.reshape(tokens, nrow, blk))
    x_sel = x_sel.astype(jnp.bfloat16)

    gu_slot = jnp.einsum("cta,cgab->ctgb", x_sel, w_pair, preferred_element_type=jnp.float32)
    gu_part = jnp.einsum("cj,ctgb->gtjb", col_f, gu_slot, precision=HOT)
    head_hi = head_sel.astype(jnp.bfloat16)
    head_lo = (head_sel - head_hi.astype(jnp.float32)).astype(jnp.bfloat16)
    head_two = jnp.stack([head_hi, head_lo], axis=1)
    folded = jnp.einsum(
        "chd,ckd->chk", w_down, head_two, preferred_element_type=jnp.float32
    ).sum(axis=2)
    f_part = jnp.einsum("cj,ch->jh", col_f, folded, precision=HOT)
    cols_per = sec_cols // members
    packed = gu_part.reshape(2 * tokens, members, cols_per, blk).transpose(1, 0, 2, 3)
    packed = scatter_blocks(packed, "fsdp", member, fsdp_bits)
    gate = packed[:tokens]
    up = packed[tokens:]
    f_sum = scatter_any(f_part.reshape(members, cols_per, blk), "fsdp", member, fsdp_bits)
    sig = jax.nn.sigmoid(gate)
    hidden_own = (gate * sig * up).astype(jnp.bfloat16)

    branch = jnp.einsum("tjh,jh->t", hidden_own.astype(jnp.float32), f_sum, precision=HI)
    x_term = jnp.einsum("td,d->t", x_mine.astype(jnp.float32), head_weight, precision=HI)
    branch = branch + jnp.where((section == 0) & (member == 0), x_term, 0.0)
    logits = sum_any(branch, "fsdp", fsdp_bits)
    logits = sum_any(logits, "segment", sec_bits) * width ** (-0.5)
    dlogit = jax.nn.sigmoid(logits) - labels.astype(jnp.float32)
    dout_last = (dlogit[:, None] * head_weight[None, :]).astype(jnp.bfloat16)

    def gate_grads(dhidden):
        dgate = (dhidden * up * sig * (1.0 + gate * (1.0 - sig))).astype(jnp.bfloat16)
        dup = (dhidden * gate * sig).astype(jnp.bfloat16)
        return dgate, dup

    def share(parts):
        whole = gather_any(jnp.stack(parts), "fsdp", member, fsdp_bits)
        n = len(parts)
        return whole.transpose(1, 2, 0, 3, 4).reshape(n, tokens, sec_cols, blk)

    def select_pair(dgate, dup):
        pair = jnp.stack([dgate, dup], axis=2)
        return jnp.einsum("cj,tjgb->ctgb", col_b, pair).astype(jnp.bfloat16)

    def spread_rows(d_sel):
        spread = jnp.einsum(
            "ctgb,cgab->cta", d_sel, w_pair, preferred_element_type=jnp.float32
        )
        return jnp.einsum("cr,cta->tra", row_f, spread, precision=HOT).reshape(tokens, width)

    dgate_last, dup_last = gate_grads(dlogit[:, None, None] * f_sum[None])
    shared = share([hidden_own, dgate_last, dup_last])
    hidden = shared[0]
    d_sel_last = select_pair(shared[1], shared[2])
    part_last = spread_rows(d_sel_last).reshape(members, tok_rows, width)
    rows_last = scatter_any(part_last, "fsdp", member, fsdp_bits)
    rows_last = sum_any(rows_last, "segment", sec_bits)
    rows_at = member * tok_rows
    cols_at = section * piece_width
    dout_rows = lax.dynamic_slice_in_dim(dout_last, rows_at, tok_rows, axis=0)
    grad_last = (dout_rows.astype(jnp.float32) + rows_last).astype(jnp.bfloat16)
    handed = lax.ppermute(
        grad_last, "segment", [(i, i - sections) for i in range(sections, places)]
    )
    first_rows = jnp.where(is_last, grad_last, handed)
    dout_first = gather_any(first_rows, "fsdp", member, fsdp_bits).reshape(tokens, width)

    dout_sel = jnp.einsum("cr,trd->ctd", row_b, dout_first.reshape(tokens, nrow, blk))
    dout_sel = dout_sel.astype(jnp.bfloat16)
    dh_slot = jnp.einsum("ctd,chd->cth", dout_sel, w_down, preferred_element_type=jnp.float32)
    dh_part = jnp.einsum("cj,cth->tjh", col_f, dh_slot, precision=HOT)
    dh_part = dh_part.reshape(tokens, members, cols_per, blk).transpose(1, 0, 2, 3)
    dhidden_first = scatter_blocks(dh_part, "fsdp", member, fsdp_bits)
    dgate_first, dup_first = gate_grads(dhidden_first)
    shared_first = share([dgate_first, dup_first])
    cot_sel = jnp.where(
        is_last,
        jnp.einsum("cr,trd->ctd", row_b, dout_last.reshape(tokens, nrow, blk)).astype(
            jnp.bfloat16
        ),
        dout_sel,
    )
    hid_sel = jnp.einsum("cj,tjh->cth", col_b, hidden).astype(jnp.bfloat16)
    grad_down = jnp.einsum(
        "cth,ctd->chd", hid_sel, cot_sel, preferred_element_type=jnp.float32
    ).astype(jnp.bfloat16)
    zero_bf = jnp.zeros((), jnp.bfloat16)
    grad_down = jnp.where(valid[:, None, None], grad_down, zero_bf)
    grad_down, shared_first = lax.optimization_barrier((grad_down, shared_first))
    d_sel_first = select_pair(shared_first[0], shared_first[1])
    part_first = spread_rows(d_sel_first).reshape(members, tok_rows, width)
    part_first = scatter_any(part_first, "fsdp", member, fsdp_bits)
    part_first = part_first.reshape(tok_rows, sections, piece_width).transpose(1, 0, 2)
    part_first = scatter_any(part_first, "segment", section, sec_bits)

    own_last = lax.dynamic_slice_in_dim(grad_last, cols_at, piece_width, axis=1)
    own_dout = lax.dynamic_slice(dout_first, (rows_at, cols_at), (tok_rows, piece_width))
    grad_first = (own_dout.astype(jnp.float32) + part_first).astype(jnp.bfloat16)
    input_grads = jnp.where(is_last, own_last, grad_first)

    d_sel = jnp.where(is_last, d_sel_last, d_sel_first)
    x_pair = jnp.broadcast_to(x_sel[:, None], (capacity, 2, tokens, blk))
    grad_pair = jnp.einsum(
        "cgta,cgtb->cgab", x_pair, d_sel.transpose(0, 2, 1, 3),
        preferred_element_type=jnp.float32,
    ).astype(jnp.bfloat16)
    grad_pair = jnp.where(valid[:, None, None, None], grad_pair, zero_bf)
    return (input_grads, grad_pair[:, None], grad_down[:, None])


def solution(mesh):
    return jax.shard_map(
        per_device,
        mesh=mesh,
        in_specs=(
            P(("groups", "fsdp"), "segment"),
            P("groups"),
            P(),
            P("fsdp", "segment", None, None, None),
            P("fsdp", "segment", None, None),
            P(),
            P(),
            P(),
        ),
        out_specs=(
            P(("groups", "fsdp"), "segment"),
            P(("groups", "fsdp"), "segment", None, None, None),
            P(("groups", "fsdp"), "segment", None, None),
        ),
        check_vma=False,
    )
```

```python
import jax
import jax.numpy as jnp
from jax import lax
from jax.sharding import PartitionSpec as P

PIPE = 2
HI = lax.Precision.HIGHEST
HOT = lax.Precision.HIGH


def bits_of(size):
    return size.bit_length() - 1


def swapped(x, axis, bit):
    size = lax.axis_size(axis)
    return lax.ppermute(x, axis, [(i, i ^ (1 << bit)) for i in range(size)])


def all_sum(x, axis, levels):
    for bit in range(levels):
        x = x + swapped(x, axis, bit)
    return x


def gather_along(x, axis, index, levels, dim):
    for bit in range(levels):
        other = swapped(x, axis, bit)
        upper = (index >> bit) & 1 == 1
        x = jnp.where(
            upper,
            jnp.concatenate([other, x], axis=dim),
            jnp.concatenate([x, other], axis=dim),
        )
    return x


def scatter_along(x, axis, index, levels, dim):
    for bit in reversed(range(levels)):
        half = x.shape[dim] // 2
        upper = (index >> bit) & 1
        keep = lax.dynamic_slice_in_dim(x, upper * half, half, axis=dim)
        send = lax.dynamic_slice_in_dim(x, (1 - upper) * half, half, axis=dim)
        x = keep + swapped(send, axis, bit)
    return x


def scatter_blocks(x, axis, index, levels):
    x = x.reshape((2,) * levels + x.shape[1:])
    for bit in range(levels):
        pos = levels - 1 - bit
        mine = (index >> bit) & 1
        keep = lax.dynamic_index_in_dim(x, mine, pos, keepdims=False)
        send = lax.dynamic_index_in_dim(x, 1 - mine, pos, keepdims=False)
        x = keep + swapped(send, axis, bit)
    return x


def gather_blocks(x, axis, index, levels):
    for count, bit in enumerate(reversed(range(levels))):
        other = swapped(x, axis, bit)
        upper = (index >> bit) & 1 == 1
        x = jnp.where(
            upper, jnp.stack([other, x], axis=count), jnp.stack([x, other], axis=count)
        )
    return x.reshape((-1,) + x.shape[levels:])


DIRECT = 4


def shifted(x, axis, shift, group):
    size = lax.axis_size(axis)
    route = [(i, i - i % group + (i % group + shift) % group) for i in range(size)]
    return lax.ppermute(x, axis, route)


def scatter_any(x, axis, index, levels):
    n = 1 << levels
    if n > DIRECT:
        return scatter_blocks(x, axis, index, levels)
    total = lax.dynamic_index_in_dim(x, index, 0, keepdims=False)
    for shift in range(1, n):
        send = lax.dynamic_index_in_dim(x, (index + shift) % n, 0, keepdims=False)
        total = total + shifted(send, axis, shift, n)
    return total


def gather_any(x, axis, index, levels):
    n = 1 << levels
    if n > DIRECT:
        return gather_blocks(x, axis, index, levels)
    got = jnp.stack([x] + [shifted(x, axis, shift, n) for shift in range(1, n)])
    order = (index - jnp.arange(n, dtype=jnp.int32)) % n
    return jnp.take(got, order, axis=0)


def sum_any(x, axis, levels):
    n = 1 << levels
    if n > DIRECT:
        return all_sum(x, axis, levels)
    total = x
    for shift in range(1, n):
        total = total + shifted(x, axis, shift, n)
    return total


def per_device(
    layer_inputs, labels, head_weight, gate_up_store, down_store, kept_rows, owners, slots
):
    members = lax.axis_size("fsdp")
    places = lax.axis_size("segment")
    sections = places // PIPE
    member = lax.axis_index("fsdp")
    place = lax.axis_index("segment")
    segment = place // sections
    section = place % sections
    is_last = segment == PIPE - 1
    tok_rows, piece_width = layer_inputs.shape
    tokens = tok_rows * members
    width = piece_width * sections
    blk = gate_up_store.shape[-1]
    capacity = gate_up_store.shape[0]
    kept = kept_rows.shape[2]
    sec_cols = kept_rows.shape[1] // sections
    nrow = width // blk
    nblocks = sec_cols * kept

    first_col = section * sec_cols
    sec_rows = lax.dynamic_slice(kept_rows, (segment, first_col, 0), (1, sec_cols, kept))
    sec_owner = lax.dynamic_slice(owners, (segment, first_col, 0), (1, sec_cols, kept))
    sec_slot = lax.dynamic_slice(slots, (segment, first_col, 0), (1, sec_cols, kept))
    sec_rows = sec_rows.reshape(nblocks)
    mine = sec_owner.reshape(nblocks) == member
    block_col = jnp.arange(nblocks, dtype=jnp.int32) // kept
    hits = mine[None, :] & (
        sec_slot.reshape(nblocks)[None, :] == jnp.arange(capacity, dtype=jnp.int32)[:, None]
    )
    valid = jnp.any(hits, axis=1)
    slot_col = jnp.sum(jnp.where(hits, block_col[None, :], 0), axis=1)
    slot_row = jnp.sum(jnp.where(hits, sec_rows[None, :], 0), axis=1)
    col_hot = valid[:, None] & (slot_col[:, None] == jnp.arange(sec_cols, dtype=jnp.int32)[None, :])
    row_hot = valid[:, None] & (slot_row[:, None] == jnp.arange(nrow, dtype=jnp.int32)[None, :])
    col_f = col_hot.astype(jnp.float32)
    col_b = col_hot.astype(jnp.bfloat16)
    row_f = row_hot.astype(jnp.float32)
    row_b = row_hot.astype(jnp.bfloat16)

    w_pair = gate_up_store[:, 0]
    w_down = down_store[:, 0]

    fsdp_bits = bits_of(members)
    sec_bits = bits_of(sections)

    x_mine = gather_along(layer_inputs, "segment", section, sec_bits, 1)
    head_sel = jnp.einsum("cr,rd->cd", row_f, head_weight.reshape(nrow, blk), precision=HI)
    x_mine, head_sel = lax.optimization_barrier((x_mine, head_sel))
    x_mine = gather_any(x_mine, "fsdp", member, fsdp_bits).reshape(tokens, width)
    x_sel = jnp.einsum("cr,trb->ctb", row_b, x_mine.reshape(tokens, nrow, blk))
    x_sel = x_sel.astype(jnp.bfloat16)

    gu_slot = jnp.einsum("cta,cgab->ctgb", x_sel, w_pair, preferred_element_type=jnp.float32)
    gu_part = jnp.einsum("cj,ctgb->gtjb", col_f, gu_slot, precision=HOT)
    head_hi = head_sel.astype(jnp.bfloat16)
    head_lo = (head_sel - head_hi.astype(jnp.float32)).astype(jnp.bfloat16)
    head_two = jnp.stack([head_hi, head_lo], axis=1)
    folded = jnp.einsum(
        "chd,ckd->chk", w_down, head_two, preferred_element_type=jnp.float32
    ).sum(axis=2)
    f_part = jnp.einsum("cj,ch->jh", col_f, folded, precision=HOT)
    cols_per = sec_cols // members
    packed = gu_part.reshape(2 * tokens, members, cols_per, blk).transpose(1, 0, 2, 3)
    packed = scatter_blocks(packed, "fsdp", member, fsdp_bits)
    gate = packed[:tokens]
    up = packed[tokens:]
    f_sum = scatter_any(f_part.reshape(members, cols_per, blk), "fsdp", member, fsdp_bits)
    sig = jax.nn.sigmoid(gate)
    hidden_own = (gate * sig * up).astype(jnp.bfloat16)

    branch = jnp.einsum("tjh,jh->t", hidden_own.astype(jnp.float32), f_sum, precision=HI)
    x_term = jnp.einsum("td,d->t", x_mine.astype(jnp.float32), head_weight, precision=HI)
    branch = branch + jnp.where((section == 0) & (member == 0), x_term, 0.0)
    logits = sum_any(branch, "fsdp", fsdp_bits)
    logits = sum_any(logits, "segment", sec_bits) * width ** (-0.5)
    dlogit = jax.nn.sigmoid(logits) - labels.astype(jnp.float32)
    dout_last = (dlogit[:, None] * head_weight[None, :]).astype(jnp.bfloat16)

    def gate_grads(dhidden):
        dgate = (dhidden * up * sig * (1.0 + gate * (1.0 - sig))).astype(jnp.bfloat16)
        dup = (dhidden * gate * sig).astype(jnp.bfloat16)
        return dgate, dup

    def share(parts):
        whole = gather_blocks(jnp.stack(parts), "fsdp", member, fsdp_bits)
        n = len(parts)
        return whole.transpose(1, 2, 0, 3, 4).reshape(n, tokens, sec_cols, blk)

    def select_pair(dgate, dup):
        pair = jnp.stack([dgate, dup], axis=2)
        return jnp.einsum("cj,tjgb->ctgb", col_b, pair).astype(jnp.bfloat16)

    def spread_rows(d_sel):
        spread = jnp.einsum(
            "ctgb,cgab->cta", d_sel, w_pair, preferred_element_type=jnp.float32
        )
        return jnp.einsum("cr,cta->tra", row_f, spread, precision=HOT).reshape(tokens, width)

    dgate_last, dup_last = gate_grads(dlogit[:, None, None] * f_sum[None])
    shared = share([hidden_own, dgate_last, dup_last])
    hidden = shared[0]
    d_sel_last = select_pair(shared[1], shared[2])
    part_last = spread_rows(d_sel_last).reshape(members, tok_rows, width)
    rows_last = scatter_blocks(part_last, "fsdp", member, fsdp_bits)
    rows_last = sum_any(rows_last, "segment", sec_bits)
    rows_at = member * tok_rows
    cols_at = section * piece_width
    dout_rows = lax.dynamic_slice_in_dim(dout_last, rows_at, tok_rows, axis=0)
    grad_last = (dout_rows.astype(jnp.float32) + rows_last).astype(jnp.bfloat16)
    handed = lax.ppermute(
        grad_last, "segment", [(i, i - sections) for i in range(sections, places)]
    )
    first_rows = jnp.where(is_last, grad_last, handed)
    dout_first = gather_any(first_rows, "fsdp", member, fsdp_bits).reshape(tokens, width)

    dout_sel = jnp.einsum("cr,trd->ctd", row_b, dout_first.reshape(tokens, nrow, blk))
    dout_sel = dout_sel.astype(jnp.bfloat16)
    dh_slot = jnp.einsum("ctd,chd->cth", dout_sel, w_down, preferred_element_type=jnp.float32)
    dh_part = jnp.einsum("cj,cth->tjh", col_f, dh_slot, precision=HOT)
    dh_part = dh_part.reshape(tokens, members, cols_per, blk).transpose(1, 0, 2, 3)
    dhidden_first = scatter_blocks(dh_part, "fsdp", member, fsdp_bits)
    dgate_first, dup_first = gate_grads(dhidden_first)
    shared_first = share([dgate_first, dup_first])
    cot_sel = jnp.where(
        is_last,
        jnp.einsum("cr,trd->ctd", row_b, dout_last.reshape(tokens, nrow, blk)).astype(
            jnp.bfloat16
        ),
        dout_sel,
    )
    hid_sel = jnp.einsum("cj,tjh->cth", col_b, hidden).astype(jnp.bfloat16)
    grad_down = jnp.einsum(
        "cth,ctd->chd", hid_sel, cot_sel, preferred_element_type=jnp.float32
    ).astype(jnp.bfloat16)
    zero_bf = jnp.zeros((), jnp.bfloat16)
    grad_down = jnp.where(valid[:, None, None], grad_down, zero_bf)
    grad_down, shared_first = lax.optimization_barrier((grad_down, shared_first))
    d_sel_first = select_pair(shared_first[0], shared_first[1])
    part_first = spread_rows(d_sel_first).reshape(members, tok_rows, width)
    part_first = scatter_blocks(part_first, "fsdp", member, fsdp_bits)
    part_first = part_first.reshape(tok_rows, sections, piece_width).transpose(1, 0, 2)
    part_first = scatter_any(part_first, "segment", section, sec_bits)

    own_last = lax.dynamic_slice_in_dim(grad_last, cols_at, piece_width, axis=1)
    own_dout = lax.dynamic_slice(dout_first, (rows_at, cols_at), (tok_rows, piece_width))
    grad_first = (own_dout.astype(jnp.float32) + part_first).astype(jnp.bfloat16)
    input_grads = jnp.where(is_last, own_last, grad_first)

    d_sel = jnp.where(is_last, d_sel_last, d_sel_first)
    x_pair = jnp.broadcast_to(x_sel[:, None], (capacity, 2, tokens, blk))
    grad_pair = jnp.einsum(
        "cgta,cgtb->cgab", x_pair, d_sel.transpose(0, 2, 1, 3),
        preferred_element_type=jnp.float32,
    ).astype(jnp.bfloat16)
    grad_pair = jnp.where(valid[:, None, None, None], grad_pair, zero_bf)
    return (input_grads, grad_pair[:, None], grad_down[:, None])


def solution(mesh):
    return jax.shard_map(
        per_device,
        mesh=mesh,
        in_specs=(
            P(("groups", "fsdp"), "segment"),
            P("groups"),
            P(),
            P("fsdp", "segment", None, None, None),
            P("fsdp", "segment", None, None),
            P(),
            P(),
            P(),
        ),
        out_specs=(
            P(("groups", "fsdp"), "segment"),
            P(("groups", "fsdp"), "segment", None, None, None),
            P(("groups", "fsdp"), "segment", None, None),
        ),
        check_vma=False,
    )
```

```python
import jax
import jax.numpy as jnp
from jax import lax
from jax.sharding import PartitionSpec as P

PIPE = 2
HI = lax.Precision.HIGHEST
HOT = lax.Precision.HIGH


def bits_of(size):
    return size.bit_length() - 1


def swapped(x, axis, bit):
    size = lax.axis_size(axis)
    return lax.ppermute(x, axis, [(i, i ^ (1 << bit)) for i in range(size)])


def all_sum(x, axis, levels):
    for bit in range(levels):
        x = x + swapped(x, axis, bit)
    return x


def gather_along(x, axis, index, levels, dim):
    for bit in range(levels):
        other = swapped(x, axis, bit)
        upper = (index >> bit) & 1 == 1
        x = jnp.where(
            upper,
            jnp.concatenate([other, x], axis=dim),
            jnp.concatenate([x, other], axis=dim),
        )
    return x


def scatter_along(x, axis, index, levels, dim):
    for bit in reversed(range(levels)):
        half = x.shape[dim] // 2
        upper = (index >> bit) & 1
        keep = lax.dynamic_slice_in_dim(x, upper * half, half, axis=dim)
        send = lax.dynamic_slice_in_dim(x, (1 - upper) * half, half, axis=dim)
        x = keep + swapped(send, axis, bit)
    return x


def scatter_blocks(x, axis, index, levels):
    x = x.reshape((2,) * levels + x.shape[1:])
    for bit in range(levels):
        pos = levels - 1 - bit
        mine = (index >> bit) & 1
        keep = lax.dynamic_index_in_dim(x, mine, pos, keepdims=False)
        send = lax.dynamic_index_in_dim(x, 1 - mine, pos, keepdims=False)
        x = keep + swapped(send, axis, bit)
    return x


def gather_blocks(x, axis, index, levels):
    for count, bit in enumerate(reversed(range(levels))):
        other = swapped(x, axis, bit)
        upper = (index >> bit) & 1 == 1
        x = jnp.where(
            upper, jnp.stack([other, x], axis=count), jnp.stack([x, other], axis=count)
        )
    return x.reshape((-1,) + x.shape[levels:])


DIRECT = 4


def shifted(x, axis, shift, group):
    size = lax.axis_size(axis)
    route = [(i, i - i % group + (i % group + shift) % group) for i in range(size)]
    return lax.ppermute(x, axis, route)


def scatter_any(x, axis, index, levels):
    n = 1 << levels
    if n > DIRECT:
        return scatter_blocks(x, axis, index, levels)
    total = lax.dynamic_index_in_dim(x, index, 0, keepdims=False)
    for shift in range(1, n):
        send = lax.dynamic_index_in_dim(x, (index + shift) % n, 0, keepdims=False)
        total = total + shifted(send, axis, shift, n)
    return total


def gather_any(x, axis, index, levels):
    n = 1 << levels
    if n > DIRECT:
        return gather_blocks(x, axis, index, levels)
    got = jnp.stack([x] + [shifted(x, axis, shift, n) for shift in range(1, n)])
    order = (index - jnp.arange(n, dtype=jnp.int32)) % n
    return jnp.take(got, order, axis=0)


def sum_any(x, axis, levels):
    n = 1 << levels
    if n > DIRECT:
        return all_sum(x, axis, levels)
    total = x
    for shift in range(1, n):
        total = total + shifted(x, axis, shift, n)
    return total


def per_device(
    layer_inputs, labels, head_weight, gate_up_store, down_store, kept_rows, owners, slots
):
    members = lax.axis_size("fsdp")
    places = lax.axis_size("segment")
    sections = places // PIPE
    member = lax.axis_index("fsdp")
    place = lax.axis_index("segment")
    segment = place // sections
    section = place % sections
    is_last = segment == PIPE - 1
    tok_rows, piece_width = layer_inputs.shape
    tokens = tok_rows * members
    width = piece_width * sections
    blk = gate_up_store.shape[-1]
    capacity = gate_up_store.shape[0]
    kept = kept_rows.shape[2]
    sec_cols = kept_rows.shape[1] // sections
    nrow = width // blk
    nblocks = sec_cols * kept

    first_col = section * sec_cols
    sec_rows = lax.dynamic_slice(kept_rows, (segment, first_col, 0), (1, sec_cols, kept))
    sec_owner = lax.dynamic_slice(owners, (segment, first_col, 0), (1, sec_cols, kept))
    sec_slot = lax.dynamic_slice(slots, (segment, first_col, 0), (1, sec_cols, kept))
    sec_rows = sec_rows.reshape(nblocks)
    mine = sec_owner.reshape(nblocks) == member
    block_col = jnp.arange(nblocks, dtype=jnp.int32) // kept
    hits = mine[None, :] & (
        sec_slot.reshape(nblocks)[None, :] == jnp.arange(capacity, dtype=jnp.int32)[:, None]
    )
    valid = jnp.any(hits, axis=1)
    slot_col = jnp.sum(jnp.where(hits, block_col[None, :], 0), axis=1)
    slot_row = jnp.sum(jnp.where(hits, sec_rows[None, :], 0), axis=1)
    col_hot = valid[:, None] & (slot_col[:, None] == jnp.arange(sec_cols, dtype=jnp.int32)[None, :])
    row_hot = valid[:, None] & (slot_row[:, None] == jnp.arange(nrow, dtype=jnp.int32)[None, :])
    col_f = col_hot.astype(jnp.float32)
    col_b = col_hot.astype(jnp.bfloat16)
    row_f = row_hot.astype(jnp.float32)
    row_b = row_hot.astype(jnp.bfloat16)

    w_pair = gate_up_store[:, 0]
    w_down = down_store[:, 0]

    fsdp_bits = bits_of(members)
    sec_bits = bits_of(sections)

    x_mine = gather_along(layer_inputs, "segment", section, sec_bits, 1)
    head_sel = jnp.einsum("cr,rd->cd", row_f, head_weight.reshape(nrow, blk), precision=HI)
    x_mine, head_sel = lax.optimization_barrier((x_mine, head_sel))
    x_mine = gather_any(x_mine, "fsdp", member, fsdp_bits).reshape(tokens, width)
    x_sel = jnp.einsum("cr,trb->ctb", row_b, x_mine.reshape(tokens, nrow, blk))
    x_sel = x_sel.astype(jnp.bfloat16)

    gu_slot = jnp.einsum("cta,cgab->ctgb", x_sel, w_pair, preferred_element_type=jnp.float32)
    gu_part = jnp.einsum("cj,ctgb->gtjb", col_f, gu_slot, precision=HOT)
    head_hi = head_sel.astype(jnp.bfloat16)
    head_lo = (head_sel - head_hi.astype(jnp.float32)).astype(jnp.bfloat16)
    head_two = jnp.stack([head_hi, head_lo], axis=1)
    folded = jnp.einsum(
        "chd,ckd->chk", w_down, head_two, preferred_element_type=jnp.float32
    ).sum(axis=2)
    f_part = jnp.einsum("cj,ch->jh", col_f, folded, precision=HOT)
    cols_per = sec_cols // members
    packed = gu_part.reshape(2 * tokens, members, cols_per, blk).transpose(1, 0, 2, 3)
    packed = scatter_blocks(packed, "fsdp", member, fsdp_bits)
    gate = packed[:tokens]
    up = packed[tokens:]
    f_sum = scatter_any(f_part.reshape(members, cols_per, blk), "fsdp", member, fsdp_bits)
    sig = jax.nn.sigmoid(gate)
    hidden_own = (gate * sig * up).astype(jnp.bfloat16)

    branch = jnp.einsum("tjh,jh->t", hidden_own.astype(jnp.float32), f_sum, precision=HI)
    x_term = jnp.einsum("td,d->t", x_mine.astype(jnp.float32), head_weight, precision=HI)
    branch = branch + jnp.where((section == 0) & (member == 0), x_term, 0.0)
    logits = sum_any(branch, "fsdp", fsdp_bits)
    logits = sum_any(logits, "segment", sec_bits) * width ** (-0.5)
    dlogit = jax.nn.sigmoid(logits) - labels.astype(jnp.float32)
    dout_last = (dlogit[:, None] * head_weight[None, :]).astype(jnp.bfloat16)

    def gate_grads(dhidden):
        dgate = (dhidden * up * sig * (1.0 + gate * (1.0 - sig))).astype(jnp.bfloat16)
        dup = (dhidden * gate * sig).astype(jnp.bfloat16)
        return dgate, dup

    def share(parts):
        whole = gather_blocks(jnp.stack(parts), "fsdp", member, fsdp_bits)
        n = len(parts)
        return whole.transpose(1, 2, 0, 3, 4).reshape(n, tokens, sec_cols, blk)

    def select_pair(dgate, dup):
        pair = jnp.stack([dgate, dup], axis=2)
        return jnp.einsum("cj,tjgb->ctgb", col_b, pair).astype(jnp.bfloat16)

    def spread_rows(d_sel):
        spread = jnp.einsum(
            "ctgb,cgab->cta", d_sel, w_pair, preferred_element_type=jnp.float32
        )
        return jnp.einsum("cr,cta->tra", row_f, spread, precision=HOT).reshape(tokens, width)

    dgate_last, dup_last = gate_grads(dlogit[:, None, None] * f_sum[None])
    shared = share([hidden_own, dgate_last, dup_last])
    hidden = shared[0]
    d_sel_last = select_pair(shared[1], shared[2])
    part_last = spread_rows(d_sel_last).reshape(members, tok_rows, width)
    rows_last = scatter_any(part_last, "fsdp", member, fsdp_bits)
    rows_last = sum_any(rows_last, "segment", sec_bits)
    rows_at = member * tok_rows
    cols_at = section * piece_width
    dout_rows = lax.dynamic_slice_in_dim(dout_last, rows_at, tok_rows, axis=0)
    grad_last = (dout_rows.astype(jnp.float32) + rows_last).astype(jnp.bfloat16)
    handed = lax.ppermute(
        grad_last, "segment", [(i, i - sections) for i in range(sections, places)]
    )
    first_rows = jnp.where(is_last, grad_last, handed)
    dout_first = gather_any(first_rows, "fsdp", member, fsdp_bits).reshape(tokens, width)

    dout_sel = jnp.einsum("cr,trd->ctd", row_b, dout_first.reshape(tokens, nrow, blk))
    dout_sel = dout_sel.astype(jnp.bfloat16)
    dh_slot = jnp.einsum("ctd,chd->cth", dout_sel, w_down, preferred_element_type=jnp.float32)
    dh_part = jnp.einsum("cj,cth->tjh", col_f, dh_slot, precision=HOT)
    dh_part = dh_part.reshape(tokens, members, cols_per, blk).transpose(1, 0, 2, 3)
    dhidden_first = scatter_blocks(dh_part, "fsdp", member, fsdp_bits)
    dgate_first, dup_first = gate_grads(dhidden_first)
    shared_first = share([dgate_first, dup_first])
    cot_sel = jnp.where(
        is_last,
        jnp.einsum("cr,trd->ctd", row_b, dout_last.reshape(tokens, nrow, blk)).astype(
            jnp.bfloat16
        ),
        dout_sel,
    )
    hid_sel = jnp.einsum("cj,tjh->cth", col_b, hidden).astype(jnp.bfloat16)
    grad_down = jnp.einsum(
        "cth,ctd->chd", hid_sel, cot_sel, preferred_element_type=jnp.float32
    ).astype(jnp.bfloat16)
    zero_bf = jnp.zeros((), jnp.bfloat16)
    grad_down = jnp.where(valid[:, None, None], grad_down, zero_bf)
    grad_down, shared_first = lax.optimization_barrier((grad_down, shared_first))
    d_sel_first = select_pair(shared_first[0], shared_first[1])
    part_first = spread_rows(d_sel_first).reshape(members, tok_rows, width)
    part_first = scatter_any(part_first, "fsdp", member, fsdp_bits)
    part_first = part_first.reshape(tok_rows, sections, piece_width).transpose(1, 0, 2)
    part_first = scatter_any(part_first, "segment", section, sec_bits)

    own_last = lax.dynamic_slice_in_dim(grad_last, cols_at, piece_width, axis=1)
    own_dout = lax.dynamic_slice(dout_first, (rows_at, cols_at), (tok_rows, piece_width))
    grad_first = (own_dout.astype(jnp.float32) + part_first).astype(jnp.bfloat16)
    input_grads = jnp.where(is_last, own_last, grad_first)

    d_sel = jnp.where(is_last, d_sel_last, d_sel_first)
    x_pair = jnp.broadcast_to(x_sel[:, None], (capacity, 2, tokens, blk))
    grad_pair = jnp.einsum(
        "cgta,cgtb->cgab", x_pair, d_sel.transpose(0, 2, 1, 3),
        preferred_element_type=jnp.float32,
    ).astype(jnp.bfloat16)
    grad_pair = jnp.where(valid[:, None, None, None], grad_pair, zero_bf)
    return (input_grads, grad_pair[:, None], grad_down[:, None])


def solution(mesh):
    return jax.shard_map(
        per_device,
        mesh=mesh,
        in_specs=(
            P(("groups", "fsdp"), "segment"),
            P("groups"),
            P(),
            P("fsdp", "segment", None, None, None),
            P("fsdp", "segment", None, None),
            P(),
            P(),
            P(),
        ),
        out_specs=(
            P(("groups", "fsdp"), "segment"),
            P(("groups", "fsdp"), "segment", None, None, None),
            P(("groups", "fsdp"), "segment", None, None),
        ),
        check_vma=False,
    )
```
